128 devices in a mesh: gx: 16 (over x, y), gy: 8 (over z, core).
Axes of the slice: x: 4, y: 4, z: 4, core: 2. Of those that a mesh axis runs over, the one named last changes fastest.
Arguments:
- start_block: float32 [8, 8, 1024, 1024], P(None, None, 'gx', 'gy'), may hold values from -120 to 120
- conductivity: float32 [8, 1024, 1024], P(None, 'gx', 'gy'), may hold values from 0.5 to 2
- reaction: float32 [8, 1024, 1024], P(None, 'gx', 'gy'), may hold values from 0.5 to 2
Outputs:
- basis: float32 [40, 8, 1024, 1024], P(None, None, 'gx', 'gy')
- r_factor: float32 [40, 40], replicated
- first_factor: float32 [40, 40], replicated
The draws below stay inside these ranges and needn't reach their ends.
All inputs are finite; a program needn't handle non-finite values.
Results may differ from the reference program's by a relative error of at most 0.00045.
Values sent between devices are 32-bit elements; how exact they have to be, the bound alone decides.
No kernel may reach another device: no remote copies, remote signals or barrier semaphores. Data moves between devices by JAX's collectives and lax.ppermute only.
A program may use at most 128 MiB of HBM per device.

```python
import math
import jax
import jax.numpy as jnp
from jax import lax

RHS = 8
STEPS = 4
NZ = 8
COLS = 40
NX = 1024
NY = 1024
CELLS = 8388608


def draw_start_block(key, part):
    key_scale = jax.random.fold_in(key, 11)
    key_rough = jax.random.fold_in(key, 12)
    key_common = jax.random.fold_in(key, 13)
    full_shape = (RHS, NZ, NX, NY)
    row_scale = jnp.exp(jax.random.uniform(key_scale, (1, NZ, NX, NY), jnp.float32, 0.0, math.log(10.0)))
    ramp_x = 1.0 + 2.0 * jnp.arange(NX, dtype=jnp.float32).reshape(1, 1, NX, 1) / max(NX - 1, 1)
    rough_part = jnp.clip(jax.random.normal(key_rough, full_shape, jnp.float32), -4.0, 4.0)
    common = jnp.clip(jax.random.normal(key_common, (1, NZ, NX, NY), jnp.float32), -4.0, 4.0)
    return 0.2 * (rough_part + 4.0 * common) * row_scale * ramp_x


def block_scale(key, extent, shards, smallest, largest):
    def one(dim, parts):
        heights = jax.random.uniform(jax.random.fold_in(jax.random.fold_in(key, 6), dim), (parts,), jnp.float32, smallest / len(shards), largest / len(shards))
        return jnp.repeat(jnp.exp(heights), extent[dim] // parts).reshape((-1,) + (1,) * (len(extent) - dim - 1))

    level = one(*shards[0])
    for cut in shards[1:]:
        level = level * one(*cut)
    return level


def setup_inputs(seed: int = 0) -> dict:
    key_list = jax.random.split(jax.random.key(seed), 4)
    return {
        "start_block": draw_start_block(jax.random.fold_in(key_list[3], 71), 0),
        "conductivity": jnp.clip(jnp.exp(math.log(2.0) - 1.3862944 * jax.random.uniform(key_list[1], (NZ, NX, NY), jnp.float32) ** block_scale(key_list[1], (NZ, NX, NY), ((1, 16), (2, 8)), -0.2, 0.2)), 0.5, 2.0),
        "reaction": jnp.clip(jnp.exp(math.log(2.0) - 1.3862944 * jax.random.uniform(key_list[2], (NZ, NX, NY), jnp.float32) ** block_scale(key_list[2], (NZ, NX, NY), ((1, 16), (2, 8)), -0.2, 0.2)), 0.5, 2.0),
    }


center_shift = 7.0
step_scale = 1.0 / 3.0

def apply_basis_map(current, conductivity, reaction):
    running = jnp.zeros_like(current)
    for along_axis, offset in ((2, -1), (2, 1), (3, -1), (3, 1), (1, -1), (1, 1)):
        beside = jnp.roll(current, offset, along_axis)
        weight = 0.5 * (conductivity + jnp.roll(conductivity, offset, along_axis - 1))
        running = running + weight * (current - beside)
    return (reaction * current + running - center_shift * current) * step_scale

def cholesky_pass(matrix, cells_total):
    gram_one = jnp.dot(matrix.astype(jnp.float32), matrix.T.astype(jnp.float32), precision=lax.Precision.HIGHEST, preferred_element_type=jnp.float32) / cells_total
    lower_one = jnp.linalg.cholesky(gram_one)
    solved = jax.scipy.linalg.solve_triangular(lower_one, matrix, lower=True)
    return (solved, lower_one)

def reference(start_block, conductivity, reaction):
    blocks = [start_block]
    for power in range(STEPS):
        blocks.append(apply_basis_map(blocks[-1], conductivity, reaction))
    krylov = jnp.concatenate(blocks, 0).reshape(COLS, CELLS)
    first_q, lower_first = cholesky_pass(krylov, CELLS)
    basis, lower_second = cholesky_pass(first_q, CELLS)
    r_factor = jnp.dot(lower_second.T.astype(jnp.float32), lower_first.T.astype(jnp.float32), precision=lax.Precision.HIGHEST, preferred_element_type=jnp.float32)
    return (basis.reshape(COLS, NZ, NX, NY), r_factor, lower_first.T)
```

```python
import jax
import jax.numpy as jnp
from jax import lax
from jax.sharding import PartitionSpec as P

STEPS = 4
COLS = 40


center_shift = 7.0
step_scale = 1.0 / 3.0


def with_halo(array, sides, width):
    for axis, dim in sides:
        count, length = (lax.axis_size(axis), array.shape[dim])
        up = [(i, (i + 1) % count) for i in range(count)]
        down = [(j, i) for i, j in up]
        last = lax.slice_in_dim(array, length - width, length, axis=dim)
        leading = lax.slice_in_dim(array, 0, width, axis=dim)
        before = lax.ppermute(last, axis, up)
        after = lax.ppermute(leading, axis, down)
        array = jnp.concatenate([before, array, after], axis=dim)
    return array


def tree_sum(value, axes):
    for axis in axes:
        count = lax.axis_size(axis)
        stride = 1
        while stride < count:
            pairs = [(i, i ^ stride) for i in range(count)]
            value = value + lax.ppermute(value, axis, pairs)
            stride *= 2
    return value


def local_apply(padded, coef, reaction_center):
    center = padded[:, :, 1:-1, 1:-1]
    coef_center = coef[:, 1:-1, 1:-1]
    neighbours = (
        (padded[:, :, 2:, 1:-1], coef[:, 2:, 1:-1]),
        (padded[:, :, :-2, 1:-1], coef[:, :-2, 1:-1]),
        (padded[:, :, 1:-1, 2:], coef[:, 1:-1, 2:]),
        (padded[:, :, 1:-1, :-2], coef[:, 1:-1, :-2]),
        (jnp.roll(center, -1, 1), jnp.roll(coef_center, -1, 0)),
        (jnp.roll(center, 1, 1), jnp.roll(coef_center, 1, 0)),
    )
    running = jnp.zeros_like(center)
    for beside, coef_beside in neighbours:
        weight = 0.5 * (coef_center + coef_beside)
        running = running + weight * (center - beside)
    return (reaction_center * center + running - center_shift * center) * step_scale


def body(start_block, conductivity, reaction):
    cells_total = (
        start_block.shape[1]
        * start_block.shape[2]
        * start_block.shape[3]
        * lax.axis_size("gx")
        * lax.axis_size("gy")
    )
    blocks = []

    def record(new_block):
        blocks.append(new_block)

    record(start_block)
    padded_coef = with_halo(conductivity, (("gx", 1), ("gy", 2)), 1)
    for power in range(STEPS):
        padded = with_halo(blocks[-1], (("gx", 2), ("gy", 3)), 1)
        record(local_apply(padded, padded_coef, reaction))
    krylov = jnp.concatenate(blocks, 0).reshape(COLS, -1)
    local_gram = jnp.dot(
        krylov, krylov.T, precision=lax.Precision.HIGHEST, preferred_element_type=jnp.float32
    )
    gram_first = tree_sum(local_gram, ("gx", "gy"))
    gram_first = gram_first / cells_total
    lower_first = jnp.linalg.cholesky(gram_first)
    first_q = jax.scipy.linalg.solve_triangular(lower_first, krylov, lower=True)
    local_again = jnp.dot(
        first_q, first_q.T, precision=lax.Precision.HIGHEST, preferred_element_type=jnp.float32
    )
    gram_second = tree_sum(local_again, ("gx", "gy")) / cells_total
    lower_second = jnp.linalg.cholesky(gram_second)
    basis = jax.scipy.linalg.solve_triangular(lower_second, first_q, lower=True)
    r_factor = jnp.dot(
        lower_second.T,
        lower_first.T,
        precision=lax.Precision.HIGHEST,
        preferred_element_type=jnp.float32,
    )
    return (
        basis.reshape(COLS, start_block.shape[1], start_block.shape[2], start_block.shape[3]),
        r_factor,
        lower_first.T,
    )


def solution(mesh):
    return jax.shard_map(
        body,
        mesh=mesh,
        in_specs=(P(None, None, "gx", "gy"), P(None, "gx", "gy"), P(None, "gx", "gy")),
        out_specs=(P(None, None, "gx", "gy"), P(), P()),
        check_vma=False,
    )
```

```python
import jax
import jax.numpy as jnp
from jax import lax
from jax.sharding import PartitionSpec as P
from jax.experimental import pallas as pl
from jax.experimental.pallas import tpu as pltpu

STEPS = 4
COLS = 40


center_shift = 7.0
step_scale = 1.0 / 3.0


HALO = 4
LANES = 256


def exchange(array, axis, dim, width):
    count, length = (lax.axis_size(axis), array.shape[dim])
    to_next = [(i, (i + 1) % count) for i in range(count)]
    to_prev = [(j, i) for i, j in to_next]
    leading = lax.slice_in_dim(array, 0, width, axis=dim)
    last = lax.slice_in_dim(array, length - width, length, axis=dim)
    if dim == array.ndim - 1:
        leading, last = (jnp.swapaxes(leading, -1, -2), jnp.swapaxes(last, -1, -2))
    from_next = lax.ppermute(leading, axis, to_prev)
    from_prev = lax.ppermute(last, axis, to_next)
    if dim == array.ndim - 1:
        from_next, from_prev = (jnp.swapaxes(from_next, -1, -2), jnp.swapaxes(from_prev, -1, -2))
    return (from_next, from_prev)


def padded_fields(start_block, conductivity, reaction):
    rhs, depth, rows, cols = start_block.shape
    packed = jnp.concatenate(
        [start_block.reshape(rhs * depth, rows, cols), conductivity, reaction], axis=0
    )
    from_next, from_prev = exchange(packed, "gx", 1, HALO)
    packed = jnp.concatenate([packed, from_next, from_prev], axis=1)
    from_next, from_prev = exchange(packed, "gy", 2, HALO)
    gap = jnp.zeros(packed.shape[:2] + (LANES - cols - 2 * HALO,), packed.dtype)
    packed = jnp.concatenate([packed, from_next, gap, from_prev], axis=2)
    planes = rhs * depth
    return (
        packed[:planes].reshape(rhs, depth, rows + 2 * HALO, LANES),
        packed[planes : planes + depth],
        packed[planes + depth :],
    )


def tree_sum(value, axes):
    for axis in axes:
        count = lax.axis_size(axis)
        stride = 1
        while stride < count:
            pairs = [(i, i ^ stride) for i in range(count)]
            value = value + lax.ppermute(value, axis, pairs)
            stride *= 2
    return value


def neighbour(value, direction):
    axis, offset = direction
    if axis == 0:
        count = value.shape[0]
        cut = offset % count
        return jnp.concatenate([value[cut:], value[:cut]], axis=0)
    return pltpu.roll(value, (-offset) % value.shape[axis], axis)


DIRECTIONS = ((1, 1), (1, -1), (2, 1), (2, -1), (0, 1), (0, -1))


def powers_kernel(block_ref, coef_ref, react_ref, out_ref, weight_ref):
    depth, rows, cols = (out_ref.shape[2], out_ref.shape[3], out_ref.shape[4])

    @pl.when(pl.program_id(0) == 0)
    def _():
        coef = coef_ref[...]
        for d, direction in enumerate(DIRECTIONS):
            weight_ref[d] = 0.5 * (coef + neighbour(coef, direction))

    current = block_ref[0]
    out_ref[0, 0] = current[:, :rows, :cols]
    react = react_ref[...]
    for power in range(1, STEPS + 1):
        running = jnp.zeros_like(current)
        for d, direction in enumerate(DIRECTIONS):
            beside = neighbour(current, direction)
            running = running + weight_ref[d] * (current - beside)
        current = (react * current + running - center_shift * current) * step_scale
        out_ref[power, 0] = current[:, :rows, :cols]


def krylov_powers(block_p, coef_p, react_p, rows, cols):
    rhs, depth, prow, lanes = block_p.shape
    return pl.pallas_call(
        powers_kernel,
        grid=(rhs,),
        in_specs=[
            pl.BlockSpec((1, depth, prow, lanes), lambda r: (r, 0, 0, 0)),
            pl.BlockSpec((depth, prow, lanes), lambda r: (0, 0, 0)),
            pl.BlockSpec((depth, prow, lanes), lambda r: (0, 0, 0)),
        ],
        out_specs=pl.BlockSpec((STEPS + 1, 1, depth, rows, cols), lambda r: (0, r, 0, 0, 0)),
        out_shape=jax.ShapeDtypeStruct((STEPS + 1, rhs, depth, rows, cols), jnp.float32),
        scratch_shapes=[pltpu.VMEM((len(DIRECTIONS), depth, prow, lanes), jnp.float32)],
        compiler_params=pltpu.CompilerParams(dimension_semantics=("arbitrary",)),
    )(block_p, coef_p, react_p)


def body(start_block, conductivity, reaction):
    cells_total = (
        start_block.shape[1]
        * start_block.shape[2]
        * start_block.shape[3]
        * lax.axis_size("gx")
        * lax.axis_size("gy")
    )
    rhs, depth, rows, cols = start_block.shape
    block_p, coef_p, react_p = padded_fields(start_block, conductivity, reaction)
    krylov = krylov_powers(block_p, coef_p, react_p, rows, cols).reshape(COLS, -1)
    local_gram = jnp.dot(
        krylov, krylov.T, precision=lax.Precision.HIGHEST, preferred_element_type=jnp.float32
    )
    gram_first = tree_sum(local_gram, ("gx", "gy"))
    gram_first = gram_first / cells_total
    lower_first = jnp.linalg.cholesky(gram_first)
    first_q = jax.scipy.linalg.solve_triangular(lower_first, krylov, lower=True)
    local_again = jnp.dot(
        first_q, first_q.T, precision=lax.Precision.HIGHEST, preferred_element_type=jnp.float32
    )
    gram_second = tree_sum(local_again, ("gx", "gy")) / cells_total
    lower_second = jnp.linalg.cholesky(gram_second)
    basis = jax.scipy.linalg.solve_triangular(lower_second, first_q, lower=True)
    r_factor = jnp.dot(
        lower_second.T,
        lower_first.T,
        precision=lax.Precision.HIGHEST,
        preferred_element_type=jnp.float32,
    )
    return (
        basis.reshape(COLS, start_block.shape[1], start_block.shape[2], start_block.shape[3]),
        r_factor,
        lower_first.T,
    )


def solution(mesh):
    return jax.shard_map(
        body,
        mesh=mesh,
        in_specs=(P(None, None, "gx", "gy"), P(None, "gx", "gy"), P(None, "gx", "gy")),
        out_specs=(P(None, None, "gx", "gy"), P(), P()),
        check_vma=False,
    )
```

```python
import jax
import jax.numpy as jnp
from jax import lax
from jax.sharding import PartitionSpec as P
from jax.experimental import pallas as pl
from jax.experimental.pallas import tpu as pltpu

STEPS = 4
COLS = 40


center_shift = 7.0
step_scale = 1.0 / 3.0


HALO = 4
LANES = 256


def edge_rows(start_block, conductivity, reaction, lo, hi):
    rhs, depth, rows, cols = start_block.shape
    return jnp.concatenate(
        [
            start_block[:, :, lo:hi].reshape(rhs * depth, hi - lo, cols),
            conductivity[:, lo:hi],
            reaction[:, lo:hi],
        ],
        axis=0,
    )


def shift_pairs(axis):
    count = lax.axis_size(axis)
    to_next = [(i, (i + 1) % count) for i in range(count)]
    return (to_next, [(j, i) for i, j in to_next])


def tall_plane(core, from_next, from_prev):
    return jnp.concatenate([core, from_next, from_prev], axis=0)


def columns_kernel(block_ref, coef_ref, react_ref, xn_ref, xp_ref, first_ref, last_ref):
    rhs, depth, rows, cols = block_ref.shape
    width = xn_ref.shape[1]
    fill = jnp.zeros((cols - rows - 2 * width, cols), jnp.float32)

    def one(plane, core):
        tall = tall_plane(core, xn_ref[plane], xp_ref[plane])
        turned = jnp.concatenate([tall, fill], axis=0).T
        first_ref[plane] = turned[:width]
        last_ref[plane] = turned[cols - width :]

    def block_plane(p, carry):
        one(p, block_ref[p // depth, p % depth])
        return carry

    def coef_plane(z, carry):
        one(rhs * depth + z, coef_ref[z])
        one(rhs * depth + depth + z, react_ref[z])
        return carry

    lax.fori_loop(0, rhs * depth, block_plane, 0)
    lax.fori_loop(0, depth, coef_plane, 0)


def edge_columns(start_block, conductivity, reaction, x_next, x_prev):
    planes, width, cols = x_next.shape
    whole = lambda shape: pl.BlockSpec(shape, lambda: (0,) * len(shape))
    strip = jax.ShapeDtypeStruct((planes, width, cols), jnp.float32)
    return pl.pallas_call(
        columns_kernel,
        in_specs=[
            whole(start_block.shape),
            whole(conductivity.shape),
            whole(reaction.shape),
            whole(x_next.shape),
            whole(x_prev.shape),
        ],
        out_specs=[whole(strip.shape), whole(strip.shape)],
        out_shape=[strip, strip],
    )(start_block, conductivity, reaction, x_next, x_prev)


def halo_strips(start_block, conductivity, reaction):
    rows = start_block.shape[2]
    x_next_pairs, x_prev_pairs = shift_pairs("gx")
    first = edge_rows(start_block, conductivity, reaction, 0, HALO)
    last = edge_rows(start_block, conductivity, reaction, rows - HALO, rows)
    x_next = lax.ppermute(first, "gx", x_prev_pairs)
    x_prev = lax.ppermute(last, "gx", x_next_pairs)
    first, last = edge_columns(start_block, conductivity, reaction, x_next, x_prev)
    y_next_pairs, y_prev_pairs = shift_pairs("gy")
    y_next = lax.ppermute(first, "gy", y_prev_pairs)
    y_prev = lax.ppermute(last, "gy", y_next_pairs)
    return (x_next, x_prev, y_next, y_prev)


def padded_plane(core, xn, xp, yn, yp):
    cols = core.shape[-1]
    width = yn.shape[0]
    tall = tall_plane(core, xn, xp)
    gap = jnp.zeros((cols - 2 * width, cols), jnp.float32)
    side = jnp.concatenate([yn, gap, yp], axis=0).T[: tall.shape[0]]
    return jnp.concatenate([tall, side], axis=1)


def tree_sum(value, axes):
    for axis in axes:
        count = lax.axis_size(axis)
        stride = 1
        while stride < count:
            pairs = [(i, i ^ stride) for i in range(count)]
            value = value + lax.ppermute(value, axis, pairs)
            stride *= 2
    return value


def neighbour(value, direction):
    axis, offset = direction
    if axis == 0:
        count = value.shape[0]
        cut = offset % count
        return jnp.concatenate([value[cut:], value[:cut]], axis=0)
    return pltpu.roll(value, (-offset) % value.shape[axis], axis)


DIRECTIONS = ((1, 1), (1, -1), (2, 1), (2, -1), (0, 1), (0, -1))


def powers_kernel(*refs):
    block_ref, coef_ref, react_ref = refs[:3]
    strips = refs[3:15]
    out_ref, weight_ref, react_pad_ref = refs[15:]
    depth, rows, cols = (out_ref.shape[2], out_ref.shape[3], out_ref.shape[4])

    def planes(core_of, group):
        sides = [strips[4 * group + k] for k in range(4)]
        return jnp.stack(
            [padded_plane(core_of(z), *(side[z] for side in sides)) for z in range(depth)], axis=0
        )

    @pl.when(pl.program_id(0) == 0)
    def _():
        coef = planes(lambda z: coef_ref[z], 1)
        for d, direction in enumerate(DIRECTIONS):
            weight_ref[d] = 0.5 * (coef + neighbour(coef, direction))
        react_pad_ref[...] = planes(lambda z: react_ref[z], 2)

    out_ref[0, 0] = block_ref[0]
    current = planes(lambda z: block_ref[0, z], 0)
    react = react_pad_ref[...]
    for power in range(1, STEPS + 1):
        running = jnp.zeros_like(current)
        for d, direction in enumerate(DIRECTIONS):
            beside = neighbour(current, direction)
            running = running + weight_ref[d] * (current - beside)
        current = (react * current + running - center_shift * current) * step_scale
        out_ref[power, 0] = current[:, :rows, :cols]


def krylov_powers(start_block, conductivity, reaction, strips):
    rhs, depth, rows, cols = start_block.shape
    width = strips[0].shape[1]
    strip_specs = []
    for group in (lambda r: r, lambda r: rhs, lambda r: rhs + 1):
        for _ in strips:
            strip_specs.append(pl.BlockSpec((depth, width, cols), lambda r, g=group: (g(r), 0, 0)))
    return pl.pallas_call(
        powers_kernel,
        grid=(rhs,),
        in_specs=[
            pl.BlockSpec((1, depth, rows, cols), lambda r: (r, 0, 0, 0)),
            pl.BlockSpec((depth, rows, cols), lambda r: (0, 0, 0)),
            pl.BlockSpec((depth, rows, cols), lambda r: (0, 0, 0)),
        ]
        + strip_specs,
        out_specs=pl.BlockSpec((STEPS + 1, 1, depth, rows, cols), lambda r: (0, r, 0, 0, 0)),
        out_shape=jax.ShapeDtypeStruct((STEPS + 1, rhs, depth, rows, cols), jnp.float32),
        scratch_shapes=[
            pltpu.VMEM((len(DIRECTIONS), depth, rows + 2 * width, LANES), jnp.float32),
            pltpu.VMEM((depth, rows + 2 * width, LANES), jnp.float32),
        ],
        compiler_params=pltpu.CompilerParams(dimension_semantics=("arbitrary",)),
    )(start_block, conductivity, reaction, *(strips * 3))


def body(start_block, conductivity, reaction):
    cells_total = (
        start_block.shape[1]
        * start_block.shape[2]
        * start_block.shape[3]
        * lax.axis_size("gx")
        * lax.axis_size("gy")
    )
    rhs, depth, rows, cols = start_block.shape
    strips = halo_strips(start_block, conductivity, reaction)
    krylov = krylov_powers(start_block, conductivity, reaction, strips).reshape(COLS, -1)
    local_gram = jnp.dot(
        krylov, krylov.T, precision=lax.Precision.HIGHEST, preferred_element_type=jnp.float32
    )
    gram_first = tree_sum(local_gram, ("gx", "gy"))
    gram_first = gram_first / cells_total
    lower_first = jnp.linalg.cholesky(gram_first)
    first_q = jax.scipy.linalg.solve_triangular(lower_first, krylov, lower=True)
    local_again = jnp.dot(
        first_q, first_q.T, precision=lax.Precision.HIGHEST, preferred_element_type=jnp.float32
    )
    gram_second = tree_sum(local_again, ("gx", "gy")) / cells_total
    lower_second = jnp.linalg.cholesky(gram_second)
    basis = jax.scipy.linalg.solve_triangular(lower_second, first_q, lower=True)
    r_factor = jnp.dot(
        lower_second.T,
        lower_first.T,
        precision=lax.Precision.HIGHEST,
        preferred_element_type=jnp.float32,
    )
    return (
        basis.reshape(COLS, start_block.shape[1], start_block.shape[2], start_block.shape[3]),
        r_factor,
        lower_first.T,
    )


def solution(mesh):
    return jax.shard_map(
        body,
        mesh=mesh,
        in_specs=(P(None, None, "gx", "gy"), P(None, "gx", "gy"), P(None, "gx", "gy")),
        out_specs=(P(None, None, "gx", "gy"), P(), P()),
        check_vma=False,
    )
```

```python
import jax
import jax.numpy as jnp
from jax import lax
from jax.sharding import PartitionSpec as P
from jax.experimental import pallas as pl
from jax.experimental.pallas import tpu as pltpu

STEPS = 4
COLS = 40


center_shift = 7.0
step_scale = 1.0 / 3.0


HALO = 4
LANES = 256


def edge_rows(start_block, conductivity, reaction, lo, hi):
    rhs, depth, rows, cols = start_block.shape
    return jnp.concatenate(
        [
            start_block[:, :, lo:hi].reshape(rhs * depth, hi - lo, cols),
            conductivity[:, lo:hi],
            reaction[:, lo:hi],
        ],
        axis=0,
    )


def shift_pairs(axis):
    count = lax.axis_size(axis)
    to_next = [(i, (i + 1) % count) for i in range(count)]
    return (to_next, [(j, i) for i, j in to_next])


def tall_plane(core, from_next, from_prev):
    return jnp.concatenate([core, from_next, from_prev], axis=0)


def columns_kernel(block_ref, coef_ref, react_ref, xn_ref, xp_ref, first_ref, last_ref):
    rhs, depth, rows, cols = block_ref.shape
    width = xn_ref.shape[1]
    fill = jnp.zeros((cols - rows - 2 * width, cols), jnp.float32)

    def one(plane, core):
        tall = tall_plane(core, xn_ref[plane], xp_ref[plane])
        turned = jnp.concatenate([tall, fill], axis=0).T
        first_ref[plane] = turned[:width]
        last_ref[plane] = turned[cols - width :]

    def block_plane(p, carry):
        one(p, block_ref[p // depth, p % depth])
        return carry

    def coef_plane(z, carry):
        one(rhs * depth + z, coef_ref[z])
        one(rhs * depth + depth + z, react_ref[z])
        return carry

    lax.fori_loop(0, rhs * depth, block_plane, 0)
    lax.fori_loop(0, depth, coef_plane, 0)


def edge_columns(start_block, conductivity, reaction, x_next, x_prev):
    planes, width, cols = x_next.shape
    whole = lambda shape: pl.BlockSpec(shape, lambda: (0,) * len(shape))
    strip = jax.ShapeDtypeStruct((planes, width, cols), jnp.float32)
    return pl.pallas_call(
        columns_kernel,
        in_specs=[
            whole(start_block.shape),
            whole(conductivity.shape),
            whole(reaction.shape),
            whole(x_next.shape),
            whole(x_prev.shape),
        ],
        out_specs=[whole(strip.shape), whole(strip.shape)],
        out_shape=[strip, strip],
    )(start_block, conductivity, reaction, x_next, x_prev)


def halo_strips(start_block, conductivity, reaction):
    rows = start_block.shape[2]
    x_next_pairs, x_prev_pairs = shift_pairs("gx")
    first = edge_rows(start_block, conductivity, reaction, 0, HALO)
    last = edge_rows(start_block, conductivity, reaction, rows - HALO, rows)
    x_next = lax.ppermute(first, "gx", x_prev_pairs)
    x_prev = lax.ppermute(last, "gx", x_next_pairs)
    first, last = edge_columns(start_block, conductivity, reaction, x_next, x_prev)
    y_next_pairs, y_prev_pairs = shift_pairs("gy")
    y_next = lax.ppermute(first, "gy", y_prev_pairs)
    y_prev = lax.ppermute(last, "gy", y_next_pairs)
    return (x_next, x_prev, y_next, y_prev)


def padded_plane(core, xn, xp, yn, yp):
    cols = core.shape[-1]
    width = yn.shape[0]
    tall = tall_plane(core, xn, xp)
    gap = jnp.zeros((cols - 2 * width, cols), jnp.float32)
    side = jnp.concatenate([yn, gap, yp], axis=0).T[: tall.shape[0]]
    return jnp.concatenate([tall, side], axis=1)


def tree_sum(value, axes):
    for axis in axes:
        count = lax.axis_size(axis)
        stride = 1
        while stride < count:
            pairs = [(i, i ^ stride) for i in range(count)]
            value = value + lax.ppermute(value, axis, pairs)
            stride *= 2
    return value


def neighbour(value, direction):
    axis, offset = direction
    if axis == 0:
        count = value.shape[0]
        cut = offset % count
        return jnp.concatenate([value[cut:], value[:cut]], axis=0)
    return pltpu.roll(value, (-offset) % value.shape[axis], axis)


DIRECTIONS = ((1, 1), (1, -1), (2, 1), (2, -1), (0, 1), (0, -1))


def powers_kernel(*refs):
    block_ref, coef_ref, react_ref = refs[:3]
    strips = refs[3:15]
    out_ref, weight_ref, react_pad_ref = refs[15:]
    depth, rows, cols = (out_ref.shape[2], out_ref.shape[3], out_ref.shape[4])

    def planes(core_of, group):
        sides = [strips[4 * group + k] for k in range(4)]
        return jnp.stack(
            [padded_plane(core_of(z), *(side[z] for side in sides)) for z in range(depth)], axis=0
        )

    @pl.when(pl.program_id(0) == 0)
    def _():
        coef = planes(lambda z: coef_ref[z], 1)
        for d, direction in enumerate(DIRECTIONS):
            weight_ref[d] = 0.5 * (coef + neighbour(coef, direction))
        react_pad_ref[...] = planes(lambda z: react_ref[z], 2)

    out_ref[0, 0] = block_ref[0]
    current = planes(lambda z: block_ref[0, z], 0)
    react = react_pad_ref[...]
    for power in range(1, STEPS + 1):
        running = jnp.zeros_like(current)
        for d, direction in enumerate(DIRECTIONS):
            beside = neighbour(current, direction)
            running = running + weight_ref[d] * (current - beside)
        current = (react * current + running - center_shift * current) * step_scale
        out_ref[power, 0] = current[:, :rows, :cols]


def krylov_powers(start_block, conductivity, reaction, strips):
    rhs, depth, rows, cols = start_block.shape
    width = strips[0].shape[1]
    strip_specs = []
    for group in (lambda r: r, lambda r: rhs, lambda r: rhs + 1):
        for _ in strips:
            strip_specs.append(pl.BlockSpec((depth, width, cols), lambda r, g=group: (g(r), 0, 0)))
    return pl.pallas_call(
        powers_kernel,
        grid=(rhs,),
        in_specs=[
            pl.BlockSpec((1, depth, rows, cols), lambda r: (r, 0, 0, 0)),
            pl.BlockSpec((depth, rows, cols), lambda r: (0, 0, 0)),
            pl.BlockSpec((depth, rows, cols), lambda r: (0, 0, 0)),
        ]
        + strip_specs,
        out_specs=pl.BlockSpec((STEPS + 1, 1, depth, rows, cols), lambda r: (0, r, 0, 0, 0)),
        out_shape=jax.ShapeDtypeStruct((STEPS + 1, rhs, depth, rows, cols), jnp.float32),
        scratch_shapes=[
            pltpu.VMEM((len(DIRECTIONS), depth, rows + 2 * width, LANES), jnp.float32),
            pltpu.VMEM((depth, rows + 2 * width, LANES), jnp.float32),
        ],
        compiler_params=pltpu.CompilerParams(dimension_semantics=("arbitrary",)),
    )(start_block, conductivity, reaction, *(strips * 3))


def body(start_block, conductivity, reaction):
    cells_total = (
        start_block.shape[1]
        * start_block.shape[2]
        * start_block.shape[3]
        * lax.axis_size("gx")
        * lax.axis_size("gy")
    )
    rhs, depth, rows, cols = start_block.shape
    strips = halo_strips(start_block, conductivity, reaction)
    krylov = krylov_powers(start_block, conductivity, reaction, strips).reshape(COLS, -1)
    local_gram = jnp.dot(
        krylov, krylov.T, precision=lax.Precision.HIGHEST, preferred_element_type=jnp.float32
    )
    gram_first = tree_sum(local_gram, ("gx", "gy"))
    gram_first = gram_first / cells_total
    lower_first = jnp.linalg.cholesky(gram_first)
    first_q = jax.scipy.linalg.solve_triangular(lower_first, krylov, lower=True)
    local_again = jnp.dot(
        first_q, first_q.T, precision=lax.Precision.HIGH, preferred_element_type=jnp.float32
    )
    gram_second = tree_sum(local_again, ("gx", "gy")) / cells_total
    lower_second = jnp.linalg.cholesky(gram_second)
    inverse = jax.scipy.linalg.solve_triangular(
        lower_second, jnp.eye(COLS, dtype=jnp.float32), lower=True
    )
    basis = jnp.dot(inverse, first_q, precision=lax.Precision.HIGH, preferred_element_type=jnp.float32)
    r_factor = jnp.dot(
        lower_second.T,
        lower_first.T,
        precision=lax.Precision.HIGHEST,
        preferred_element_type=jnp.float32,
    )
    return (
        basis.reshape(COLS, start_block.shape[1], start_block.shape[2], start_block.shape[3]),
        r_factor,
        lower_first.T,
    )


def solution(mesh):
    return jax.shard_map(
        body,
        mesh=mesh,
        in_specs=(P(None, None, "gx", "gy"), P(None, "gx", "gy"), P(None, "gx", "gy")),
        out_specs=(P(None, None, "gx", "gy"), P(), P()),
        check_vma=False,
    )
```

```python
import jax
import jax.numpy as jnp
from jax import lax
from jax.sharding import PartitionSpec as P
from jax.experimental import pallas as pl
from jax.experimental.pallas import tpu as pltpu

STEPS = 4
COLS = 40


center_shift = 7.0
step_scale = 1.0 / 3.0


HALO = 4
LANES = 256


def edge_rows(start_block, conductivity, reaction, lo, hi):
    rhs, depth, rows, cols = start_block.shape
    return jnp.concatenate(
        [
            start_block[:, :, lo:hi].reshape(rhs * depth, hi - lo, cols),
            conductivity[:, lo:hi],
            reaction[:, lo:hi],
        ],
        axis=0,
    )


def shift_pairs(axis):
    count = lax.axis_size(axis)
    to_next = [(i, (i + 1) % count) for i in range(count)]
    return (to_next, [(j, i) for i, j in to_next])


def tall_plane(core, from_next, from_prev):
    return jnp.concatenate([core, from_next, from_prev], axis=0)


def columns_kernel(block_ref, coef_ref, react_ref, xn_ref, xp_ref, first_ref, last_ref):
    rhs, depth, rows, cols = block_ref.shape
    width = xn_ref.shape[1]
    fill = jnp.zeros((cols - rows - 2 * width, cols), jnp.float32)

    def one(plane, core):
        tall = tall_plane(core, xn_ref[plane], xp_ref[plane])
        turned = jnp.concatenate([tall, fill], axis=0).T
        first_ref[plane] = turned[:width]
        last_ref[plane] = turned[cols - width :]

    def block_plane(p, carry):
        one(p, block_ref[p // depth, p % depth])
        return carry

    def coef_plane(z, carry):
        one(rhs * depth + z, coef_ref[z])
        one(rhs * depth + depth + z, react_ref[z])
        return carry

    lax.fori_loop(0, rhs * depth, block_plane, 0)
    lax.fori_loop(0, depth, coef_plane, 0)


def edge_columns(start_block, conductivity, reaction, x_next, x_prev):
    planes, width, cols = x_next.shape
    whole = lambda shape: pl.BlockSpec(shape, lambda: (0,) * len(shape))
    strip = jax.ShapeDtypeStruct((planes, width, cols), jnp.float32)
    return pl.pallas_call(
        columns_kernel,
        in_specs=[
            whole(start_block.shape),
            whole(conductivity.shape),
            whole(reaction.shape),
            whole(x_next.shape),
            whole(x_prev.shape),
        ],
        out_specs=[whole(strip.shape), whole(strip.shape)],
        out_shape=[strip, strip],
    )(start_block, conductivity, reaction, x_next, x_prev)


def halo_strips(start_block, conductivity, reaction):
    rows = start_block.shape[2]
    x_next_pairs, x_prev_pairs = shift_pairs("gx")
    first = edge_rows(start_block, conductivity, reaction, 0, HALO)
    last = edge_rows(start_block, conductivity, reaction, rows - HALO, rows)
    x_next = lax.ppermute(first, "gx", x_prev_pairs)
    x_prev = lax.ppermute(last, "gx", x_next_pairs)
    first, last = edge_columns(start_block, conductivity, reaction, x_next, x_prev)
    y_next_pairs, y_prev_pairs = shift_pairs("gy")
    y_next = lax.ppermute(first, "gy", y_prev_pairs)
    y_prev = lax.ppermute(last, "gy", y_next_pairs)
    return (x_next, x_prev, y_next, y_prev)


def padded_plane(core, xn, xp, yn, yp):
    cols = core.shape[-1]
    width = yn.shape[0]
    tall = tall_plane(core, xn, xp)
    gap = jnp.zeros((cols - 2 * width, cols), jnp.float32)
    side = jnp.concatenate([yn, gap, yp], axis=0).T[: tall.shape[0]]
    return jnp.concatenate([tall, side], axis=1)


def tree_sum(value, axes):
    for axis in axes:
        count = lax.axis_size(axis)
        stride = 1
        while stride < count:
            pairs = [(i, i ^ stride) for i in range(count)]
            value = value + lax.ppermute(value, axis, pairs)
            stride *= 2
    return value


def neighbour(value, direction):
    axis, offset = direction
    if axis == 0:
        count = value.shape[0]
        cut = offset % count
        return jnp.concatenate([value[cut:], value[:cut]], axis=0)
    return pltpu.roll(value, (-offset) % value.shape[axis], axis)


DIRECTIONS = ((1, 1), (1, -1), (2, 1), (2, -1), (0, 1), (0, -1))


def powers_kernel(*refs):
    block_ref, coef_ref, react_ref = refs[:3]
    strips = refs[3:15]
    out_ref, weight_ref, react_pad_ref = refs[15:]
    depth, rows, cols = (out_ref.shape[2], out_ref.shape[3], out_ref.shape[4])

    def planes(core_of, group):
        sides = [strips[4 * group + k] for k in range(4)]
        return jnp.stack(
            [padded_plane(core_of(z), *(side[z] for side in sides)) for z in range(depth)], axis=0
        )

    @pl.when(pl.program_id(0) == 0)
    def _():
        coef = planes(lambda z: coef_ref[z], 1)
        for d, direction in enumerate(DIRECTIONS):
            weight_ref[d] = 0.5 * (coef + neighbour(coef, direction))
        react_pad_ref[...] = planes(lambda z: react_ref[z], 2)

    out_ref[0, 0] = block_ref[0]
    current = planes(lambda z: block_ref[0, z], 0)
    react = react_pad_ref[...]
    for power in range(1, STEPS + 1):
        running = jnp.zeros_like(current)
        for d, direction in enumerate(DIRECTIONS):
            beside = neighbour(current, direction)
            running = running + weight_ref[d] * (current - beside)
        current = (react * current + running - center_shift * current) * step_scale
        out_ref[power, 0] = current[:, :rows, :cols]


def krylov_powers(start_block, conductivity, reaction, strips):
    rhs, depth, rows, cols = start_block.shape
    width = strips[0].shape[1]
    strip_specs = []
    for group in (lambda r: r, lambda r: rhs, lambda r: rhs + 1):
        for _ in strips:
            strip_specs.append(pl.BlockSpec((depth, width, cols), lambda r, g=group: (g(r), 0, 0)))
    return pl.pallas_call(
        powers_kernel,
        grid=(rhs,),
        in_specs=[
            pl.BlockSpec((1, depth, rows, cols), lambda r: (r, 0, 0, 0)),
            pl.BlockSpec((depth, rows, cols), lambda r: (0, 0, 0)),
            pl.BlockSpec((depth, rows, cols), lambda r: (0, 0, 0)),
        ]
        + strip_specs,
        out_specs=pl.BlockSpec((STEPS + 1, 1, depth, rows, cols), lambda r: (0, r, 0, 0, 0)),
        out_shape=jax.ShapeDtypeStruct((STEPS + 1, rhs, depth, rows, cols), jnp.float32),
        scratch_shapes=[
            pltpu.VMEM((len(DIRECTIONS), depth, rows + 2 * width, LANES), jnp.float32),
            pltpu.VMEM((depth, rows + 2 * width, LANES), jnp.float32),
        ],
        compiler_params=pltpu.CompilerParams(dimension_semantics=("arbitrary",)),
    )(start_block, conductivity, reaction, *(strips * 3))


def factor_kernel(gram_ref, upper_ref, inverse_ref):
    size = gram_ref.shape[0]
    rows = lax.broadcasted_iota(jnp.int32, (size, size), 0)
    cols = lax.broadcasted_iota(jnp.int32, (size, size), 1)
    work = gram_ref[...]
    lower = jnp.zeros((size, size), jnp.float32)
    upper = jnp.zeros((size, size), jnp.float32)
    for j in range(size):
        pivot = jnp.sqrt(work[j : j + 1, j : j + 1])
        column = jnp.where(rows[:, j : j + 1] >= j, work[:, j : j + 1] / pivot, 0.0)
        row = jnp.where(cols[j : j + 1, :] >= j, work[j : j + 1, :] / pivot, 0.0)
        lower = jnp.where(cols == j, column, lower)
        upper = jnp.where(rows == j, row, upper)
        work = work - column * row
    pending = jnp.where(rows == cols, 1.0, 0.0).astype(jnp.float32)
    inverse = jnp.zeros((size, size), jnp.float32)
    for k in range(size):
        solved = pending[k : k + 1, :] / lower[k : k + 1, k : k + 1]
        inverse = jnp.where(rows == k, solved, inverse)
        below = jnp.where(rows[:, k : k + 1] > k, lower[:, k : k + 1], 0.0)
        pending = pending - below * solved
    upper_ref[...] = upper
    inverse_ref[...] = inverse


def cholesky_factors(gram, cells_total):
    size = gram.shape[0]
    square = jax.ShapeDtypeStruct((size, size), jnp.float32)
    scaled = gram / cells_total
    symmetric = (scaled + scaled.T) / 2
    return pl.pallas_call(factor_kernel, out_shape=[square, square])(symmetric)


def body(start_block, conductivity, reaction):
    cells_total = (
        start_block.shape[1]
        * start_block.shape[2]
        * start_block.shape[3]
        * lax.axis_size("gx")
        * lax.axis_size("gy")
    )
    rhs, depth, rows, cols = start_block.shape
    strips = halo_strips(start_block, conductivity, reaction)
    krylov = krylov_powers(start_block, conductivity, reaction, strips).reshape(COLS, -1)
    local_gram = jnp.dot(
        krylov, krylov.T, precision=lax.Precision.HIGHEST, preferred_element_type=jnp.float32
    )
    upper_first, inverse_first = cholesky_factors(tree_sum(local_gram, ("gx", "gy")), cells_total)
    first_q = jnp.dot(
        inverse_first, krylov, precision=lax.Precision.HIGHEST, preferred_element_type=jnp.float32
    )
    local_again = jnp.dot(
        first_q, first_q.T, precision=lax.Precision.HIGH, preferred_element_type=jnp.float32
    )
    upper_second, inverse_second = cholesky_factors(tree_sum(local_again, ("gx", "gy")), cells_total)
    basis = jnp.dot(
        inverse_second, first_q, precision=lax.Precision.HIGH, preferred_element_type=jnp.float32
    )
    r_factor = jnp.dot(
        upper_second,
        upper_first,
        precision=lax.Precision.HIGHEST,
        preferred_element_type=jnp.float32,
    )
    return (
        basis.reshape(COLS, start_block.shape[1], start_block.shape[2], start_block.shape[3]),
        r_factor,
        upper_first,
    )


def solution(mesh):
    return jax.shard_map(
        body,
        mesh=mesh,
        in_specs=(P(None, None, "gx", "gy"), P(None, "gx", "gy"), P(None, "gx", "gy")),
        out_specs=(P(None, None, "gx", "gy"), P(), P()),
        check_vma=False,
    )
```

```python
import jax
import jax.numpy as jnp
from jax import lax
from jax.sharding import PartitionSpec as P
from jax.experimental import pallas as pl
from jax.experimental.pallas import tpu as pltpu

STEPS = 4
COLS = 40


center_shift = 7.0
step_scale = 1.0 / 3.0


HALO = 4
LANES = 256


def edge_rows(start_block, conductivity, reaction, lo, hi):
    rhs, depth, rows, cols = start_block.shape
    return jnp.concatenate(
        [
            start_block[:, :, lo:hi].reshape(rhs * depth, hi - lo, cols),
            conductivity[:, lo:hi],
            reaction[:, lo:hi],
        ],
        axis=0,
    )


def shift_pairs(axis):
    count = lax.axis_size(axis)
    to_next = [(i, (i + 1) % count) for i in range(count)]
    return (to_next, [(j, i) for i, j in to_next])


def tall_plane(core, from_next, from_prev):
    return jnp.concatenate([core, from_next, from_prev], axis=0)


def columns_kernel(block_ref, coef_ref, react_ref, xn_ref, xp_ref, first_ref, last_ref):
    rhs, depth, rows, cols = block_ref.shape
    width = xn_ref.shape[1]
    fill = jnp.zeros((cols - rows - 2 * width, cols), jnp.float32)

    def one(plane, core):
        tall = tall_plane(core, xn_ref[plane], xp_ref[plane])
        turned = jnp.concatenate([tall, fill], axis=0).T
        first_ref[plane] = turned[:width]
        last_ref[plane] = turned[cols - width :]

    def block_plane(p, carry):
        one(p, block_ref[p // depth, p % depth])
        return carry

    def coef_plane(z, carry):
        one(rhs * depth + z, coef_ref[z])
        one(rhs * depth + depth + z, react_ref[z])
        return carry

    lax.fori_loop(0, rhs * depth, block_plane, 0)
    lax.fori_loop(0, depth, coef_plane, 0)


def edge_columns(start_block, conductivity, reaction, x_next, x_prev):
    planes, width, cols = x_next.shape
    whole = lambda shape: pl.BlockSpec(shape, lambda: (0,) * len(shape))
    strip = jax.ShapeDtypeStruct((planes, width, cols), jnp.float32)
    return pl.pallas_call(
        columns_kernel,
        in_specs=[
            whole(start_block.shape),
            whole(conductivity.shape),
            whole(reaction.shape),
            whole(x_next.shape),
            whole(x_prev.shape),
        ],
        out_specs=[whole(strip.shape), whole(strip.shape)],
        out_shape=[strip, strip],
    )(start_block, conductivity, reaction, x_next, x_prev)


def halo_strips(start_block, conductivity, reaction):
    rows = start_block.shape[2]
    x_next_pairs, x_prev_pairs = shift_pairs("gx")
    first = edge_rows(start_block, conductivity, reaction, 0, HALO)
    last = edge_rows(start_block, conductivity, reaction, rows - HALO, rows)
    x_next = lax.ppermute(first, "gx", x_prev_pairs)
    x_prev = lax.ppermute(last, "gx", x_next_pairs)
    first, last = edge_columns(start_block, conductivity, reaction, x_next, x_prev)
    y_next_pairs, y_prev_pairs = shift_pairs("gy")
    y_next = lax.ppermute(first, "gy", y_prev_pairs)
    y_prev = lax.ppermute(last, "gy", y_next_pairs)
    return (x_next, x_prev, y_next, y_prev)


def padded_plane(core, xn, xp, yn, yp):
    cols = core.shape[-1]
    width = yn.shape[0]
    tall = tall_plane(core, xn, xp)
    gap = jnp.zeros((cols - 2 * width, cols), jnp.float32)
    side = jnp.concatenate([yn, gap, yp], axis=0).T[: tall.shape[0]]
    return jnp.concatenate([tall, side], axis=1)


def fold_pairs(count, stride, span, fold):
    pairs = []
    for i in range(count):
        place = (i // stride) % span
        other = (span - 1 - place) if fold else (place ^ 1)
        pairs.append((i, i + (other - place) * stride))
    return pairs


def ring_spans(axis):
    count = lax.axis_size(axis)
    rings = {("gx", 16): ((4, 4), (1, 4)), ("gy", 8): ((1, 2), (2, 4))}
    if (axis, count) in rings:
        return rings[(axis, count)]
    return tuple((1 << b, 2) for b in range(count.bit_length() - 1))


def tree_sum(value, axes):
    for axis in axes:
        count = lax.axis_size(axis)
        for stride, span in ring_spans(axis):
            folds = (False, True) if span == 4 else (False,)
            for fold in folds:
                value = value + lax.ppermute(value, axis, fold_pairs(count, stride, span, fold))
    return value


def neighbour(value, direction):
    axis, offset = direction
    if axis == 0:
        count = value.shape[0]
        cut = offset % count
        return jnp.concatenate([value[cut:], value[:cut]], axis=0)
    return pltpu.roll(value, (-offset) % value.shape[axis], axis)


DIRECTIONS = ((1, 1), (1, -1), (2, 1), (2, -1), (0, 1), (0, -1))


def powers_kernel(*refs):
    block_ref, coef_ref, react_ref = refs[:3]
    strips = refs[3:15]
    out_ref, weight_ref, react_pad_ref = refs[15:]
    depth, rows, cols = (out_ref.shape[2], out_ref.shape[3], out_ref.shape[4])

    def planes(core_of, group):
        sides = [strips[4 * group + k] for k in range(4)]
        return jnp.stack(
            [padded_plane(core_of(z), *(side[z] for side in sides)) for z in range(depth)], axis=0
        )

    @pl.when(pl.program_id(0) == 0)
    def _():
        coef = planes(lambda z: coef_ref[z], 1)
        for d, direction in enumerate(DIRECTIONS):
            weight_ref[d] = 0.5 * (coef + neighbour(coef, direction))
        react_pad_ref[...] = planes(lambda z: react_ref[z], 2)

    out_ref[0, 0] = block_ref[0]
    current = planes(lambda z: block_ref[0, z], 0)
    react = react_pad_ref[...]
    for power in range(1, STEPS + 1):
        running = jnp.zeros_like(current)
        for d, direction in enumerate(DIRECTIONS):
            beside = neighbour(current, direction)
            running = running + weight_ref[d] * (current - beside)
        current = (react * current + running - center_shift * current) * step_scale
        out_ref[power, 0] = current[:, :rows, :cols]


def krylov_powers(start_block, conductivity, reaction, strips):
    rhs, depth, rows, cols = start_block.shape
    width = strips[0].shape[1]
    strip_specs = []
    for group in (lambda r: r, lambda r: rhs, lambda r: rhs + 1):
        for _ in strips:
            strip_specs.append(pl.BlockSpec((depth, width, cols), lambda r, g=group: (g(r), 0, 0)))
    return pl.pallas_call(
        powers_kernel,
        grid=(rhs,),
        in_specs=[
            pl.BlockSpec((1, depth, rows, cols), lambda r: (r, 0, 0, 0)),
            pl.BlockSpec((depth, rows, cols), lambda r: (0, 0, 0)),
            pl.BlockSpec((depth, rows, cols), lambda r: (0, 0, 0)),
        ]
        + strip_specs,
        out_specs=pl.BlockSpec((STEPS + 1, 1, depth, rows, cols), lambda r: (0, r, 0, 0, 0)),
        out_shape=jax.ShapeDtypeStruct((STEPS + 1, rhs, depth, rows, cols), jnp.float32),
        scratch_shapes=[
            pltpu.VMEM((len(DIRECTIONS), depth, rows + 2 * width, LANES), jnp.float32),
            pltpu.VMEM((depth, rows + 2 * width, LANES), jnp.float32),
        ],
        compiler_params=pltpu.CompilerParams(dimension_semantics=("arbitrary",)),
    )(start_block, conductivity, reaction, *(strips * 3))


def factor_kernel(gram_ref, upper_ref, inverse_ref):
    size = gram_ref.shape[0]
    rows = lax.broadcasted_iota(jnp.int32, (size, size), 0)
    cols = lax.broadcasted_iota(jnp.int32, (size, size), 1)
    work = gram_ref[...]
    lower = jnp.zeros((size, size), jnp.float32)
    upper = jnp.zeros((size, size), jnp.float32)
    for j in range(size):
        pivot = jnp.sqrt(work[j : j + 1, j : j + 1])
        column = jnp.where(rows[:, j : j + 1] >= j, work[:, j : j + 1] / pivot, 0.0)
        row = jnp.where(cols[j : j + 1, :] >= j, work[j : j + 1, :] / pivot, 0.0)
        lower = jnp.where(cols == j, column, lower)
        upper = jnp.where(rows == j, row, upper)
        work = work - column * row
    pending = jnp.where(rows == cols, 1.0, 0.0).astype(jnp.float32)
    inverse = jnp.zeros((size, size), jnp.float32)
    for k in range(size):
        solved = pending[k : k + 1, :] / lower[k : k + 1, k : k + 1]
        inverse = jnp.where(rows == k, solved, inverse)
        below = jnp.where(rows[:, k : k + 1] > k, lower[:, k : k + 1], 0.0)
        pending = pending - below * solved
    upper_ref[...] = upper
    inverse_ref[...] = inverse


def cholesky_factors(gram, cells_total):
    size = gram.shape[0]
    square = jax.ShapeDtypeStruct((size, size), jnp.float32)
    scaled = gram / cells_total
    symmetric = (scaled + scaled.T) / 2
    return pl.pallas_call(factor_kernel, out_shape=[square, square])(symmetric)


def body(start_block, conductivity, reaction):
    cells_total = (
        start_block.shape[1]
        * start_block.shape[2]
        * start_block.shape[3]
        * lax.axis_size("gx")
        * lax.axis_size("gy")
    )
    rhs, depth, rows, cols = start_block.shape
    strips = halo_strips(start_block, conductivity, reaction)
    krylov = krylov_powers(start_block, conductivity, reaction, strips).reshape(COLS, -1)
    local_gram = jnp.dot(
        krylov, krylov.T, precision=lax.Precision.HIGHEST, preferred_element_type=jnp.float32
    )
    upper_first, inverse_first = cholesky_factors(tree_sum(local_gram, ("gx", "gy")), cells_total)
    first_q = jnp.dot(
        inverse_first, krylov, precision=lax.Precision.HIGHEST, preferred_element_type=jnp.float32
    )
    local_again = jnp.dot(
        first_q, first_q.T, precision=lax.Precision.HIGH, preferred_element_type=jnp.float32
    )
    upper_second, inverse_second = cholesky_factors(tree_sum(local_again, ("gx", "gy")), cells_total)
    basis = jnp.dot(
        inverse_second, first_q, precision=lax.Precision.HIGH, preferred_element_type=jnp.float32
    )
    r_factor = jnp.dot(
        upper_second,
        upper_first,
        precision=lax.Precision.HIGHEST,
        preferred_element_type=jnp.float32,
    )
    return (
        basis.reshape(COLS, start_block.shape[1], start_block.shape[2], start_block.shape[3]),
        r_factor,
        upper_first,
    )


def solution(mesh):
    return jax.shard_map(
        body,
        mesh=mesh,
        in_specs=(P(None, None, "gx", "gy"), P(None, "gx", "gy"), P(None, "gx", "gy")),
        out_specs=(P(None, None, "gx", "gy"), P(), P()),
        check_vma=False,
    )
```

```python
import jax
import jax.numpy as jnp
from jax import lax
from jax.sharding import PartitionSpec as P
from jax.experimental import pallas as pl
from jax.experimental.pallas import tpu as pltpu

STEPS = 4
COLS = 40


center_shift = 7.0
step_scale = 1.0 / 3.0


HALO = 4
LANES = 256


def edge_rows(start_block, conductivity, reaction, lo, hi):
    rhs, depth, rows, cols = start_block.shape
    return jnp.concatenate(
        [
            start_block[:, :, lo:hi].reshape(rhs * depth, hi - lo, cols),
            conductivity[:, lo:hi],
            reaction[:, lo:hi],
        ],
        axis=0,
    )


def shift_pairs(axis):
    count = lax.axis_size(axis)
    to_next = [(i, (i + 1) % count) for i in range(count)]
    return (to_next, [(j, i) for i, j in to_next])


def tall_plane(core, from_next, from_prev):
    return jnp.concatenate([core, from_next, from_prev], axis=0)


PACK = 32


def columns_kernel(block_ref, coef_ref, react_ref, xn_ref, xp_ref, first_ref, last_ref):
    rhs, depth, rows, cols = block_ref.shape
    width = xn_ref.shape[1]
    groups, tall_rows = first_ref.shape[:2]
    lane = lax.broadcasted_iota(jnp.int32, (tall_rows, cols), 1)
    cores = [block_ref[r, z] for r in range(rhs) for z in range(depth)]
    cores += [coef_ref[z] for z in range(depth)] + [react_ref[z] for z in range(depth)]
    for group in range(groups):
        first = jnp.zeros((tall_rows, cols), jnp.float32)
        last = jnp.zeros((tall_rows, cols), jnp.float32)
        for k in range(PACK):
            plane = group * PACK + k
            if plane >= len(cores):
                break
            tall = tall_plane(cores[plane], xn_ref[plane], xp_ref[plane])
            mine = (lane >= width * k) & (lane < width * (k + 1))
            first = jnp.where(mine, pltpu.roll(tall, width * k, 1), first)
            last = jnp.where(mine, pltpu.roll(tall, (width * (k + 1)) % cols, 1), last)
        first_ref[group] = first
        last_ref[group] = last


def edge_columns(start_block, conductivity, reaction, x_next, x_prev):
    planes, width, cols = x_next.shape
    rows = start_block.shape[2] + 2 * width
    whole = lambda shape: pl.BlockSpec(shape, lambda: (0,) * len(shape))
    strip = jax.ShapeDtypeStruct((-(-planes // PACK), rows, cols), jnp.float32)
    return pl.pallas_call(
        columns_kernel,
        in_specs=[
            whole(start_block.shape),
            whole(conductivity.shape),
            whole(reaction.shape),
            whole(x_next.shape),
            whole(x_prev.shape),
        ],
        out_specs=[whole(strip.shape), whole(strip.shape)],
        out_shape=[strip, strip],
    )(start_block, conductivity, reaction, x_next, x_prev)


def halo_strips(start_block, conductivity, reaction):
    rows = start_block.shape[2]
    x_next_pairs, x_prev_pairs = shift_pairs("gx")
    first = edge_rows(start_block, conductivity, reaction, 0, HALO)
    last = edge_rows(start_block, conductivity, reaction, rows - HALO, rows)
    x_next = lax.ppermute(first, "gx", x_prev_pairs)
    x_prev = lax.ppermute(last, "gx", x_next_pairs)
    first, last = edge_columns(start_block, conductivity, reaction, x_next, x_prev)
    y_next_pairs, y_prev_pairs = shift_pairs("gy")
    y_next = lax.ppermute(first, "gy", y_prev_pairs)
    y_prev = lax.ppermute(last, "gy", y_next_pairs)
    return (x_next, x_prev, y_next, y_prev)


def padded_plane(core, xn, xp, yn, yp, slot):
    tall = tall_plane(core, xn, xp)
    rows, cols = tall.shape
    width = xn.shape[0]
    lane = lax.broadcasted_iota(jnp.int32, (rows, cols), 1)
    from_next = pltpu.roll(yn, (cols - width * slot) % cols, 1)
    from_prev = pltpu.roll(yp, (cols - width - width * slot) % cols, 1)
    side = jnp.where(lane < width, from_next, jnp.where(lane >= cols - width, from_prev, 0.0))
    return jnp.concatenate([tall, side], axis=1)


def fold_pairs(count, stride, span, fold):
    pairs = []
    for i in range(count):
        place = (i // stride) % span
        other = (span - 1 - place) if fold else (place ^ 1)
        pairs.append((i, i + (other - place) * stride))
    return pairs


def ring_spans(axis):
    count = lax.axis_size(axis)
    rings = {("gx", 16): ((4, 4), (1, 4)), ("gy", 8): ((1, 2), (2, 4))}
    if (axis, count) in rings:
        return rings[(axis, count)]
    return tuple((1 << b, 2) for b in range(count.bit_length() - 1))


def tree_sum(value, axes):
    for axis in axes:
        count = lax.axis_size(axis)
        for stride, span in ring_spans(axis):
            folds = (False, True) if span == 4 else (False,)
            for fold in folds:
                value = value + lax.ppermute(value, axis, fold_pairs(count, stride, span, fold))
    return value


def neighbour(value, direction):
    axis, offset = direction
    if axis == 0:
        count = value.shape[0]
        cut = offset % count
        return jnp.concatenate([value[cut:], value[:cut]], axis=0)
    return pltpu.roll(value, (-offset) % value.shape[axis], axis)


DIRECTIONS = ((1, 1), (1, -1), (2, 1), (2, -1), (0, 1), (0, -1))


def powers_kernel(*refs):
    block_ref, coef_ref, react_ref = refs[:3]
    x_strips = refs[3:9]
    yn_ref, yp_ref = refs[9:11]
    out_ref, weight_ref, react_pad_ref = refs[11:]
    depth, rows, cols = (out_ref.shape[2], out_ref.shape[3], out_ref.shape[4])
    r = pl.program_id(0)

    def planes(core_of, group, first_plane):
        xn, xp = (x_strips[2 * group], x_strips[2 * group + 1])
        stacked = []
        for z in range(depth):
            plane = first_plane + z
            tile = plane // PACK
            stacked.append(
                padded_plane(core_of(z), xn[z], xp[z], yn_ref[tile], yp_ref[tile], plane % PACK)
            )
        return jnp.stack(stacked, axis=0)

    rhs = pl.num_programs(0)

    @pl.when(r == 0)
    def _():
        coef = planes(lambda z: coef_ref[z], 1, rhs * depth)
        for d, direction in enumerate(DIRECTIONS):
            weight_ref[d] = 0.5 * (coef + neighbour(coef, direction))
        react_pad_ref[...] = planes(lambda z: react_ref[z], 2, rhs * depth + depth)

    out_ref[0, 0] = block_ref[0]
    current = planes(lambda z: block_ref[0, z], 0, r * depth)
    react = react_pad_ref[...]
    for power in range(1, STEPS + 1):
        running = jnp.zeros_like(current)
        for d, direction in enumerate(DIRECTIONS):
            beside = neighbour(current, direction)
            running = running + weight_ref[d] * (current - beside)
        current = (react * current + running - center_shift * current) * step_scale
        out_ref[power, 0] = current[:, :rows, :cols]


def krylov_powers(start_block, conductivity, reaction, strips):
    rhs, depth, rows, cols = start_block.shape
    x_next, x_prev, y_next, y_prev = strips
    width = x_next.shape[1]
    strip_specs = []
    for group in (lambda r: r, lambda r: rhs, lambda r: rhs + 1):
        for _ in range(2):
            strip_specs.append(pl.BlockSpec((depth, width, cols), lambda r, g=group: (g(r), 0, 0)))
    packed = pl.BlockSpec(y_next.shape, lambda r: (0, 0, 0))
    return pl.pallas_call(
        powers_kernel,
        grid=(rhs,),
        in_specs=[
            pl.BlockSpec((1, depth, rows, cols), lambda r: (r, 0, 0, 0)),
            pl.BlockSpec((depth, rows, cols), lambda r: (0, 0, 0)),
            pl.BlockSpec((depth, rows, cols), lambda r: (0, 0, 0)),
        ]
        + strip_specs
        + [packed, packed],
        out_specs=pl.BlockSpec((STEPS + 1, 1, depth, rows, cols), lambda r: (0, r, 0, 0, 0)),
        out_shape=jax.ShapeDtypeStruct((STEPS + 1, rhs, depth, rows, cols), jnp.float32),
        scratch_shapes=[
            pltpu.VMEM((len(DIRECTIONS), depth, rows + 2 * width, LANES), jnp.float32),
            pltpu.VMEM((depth, rows + 2 * width, LANES), jnp.float32),
        ],
        compiler_params=pltpu.CompilerParams(dimension_semantics=("arbitrary",)),
    )(start_block, conductivity, reaction, *([x_next, x_prev] * 3), y_next, y_prev)


def factor_kernel(gram_ref, upper_ref, inverse_ref):
    size = gram_ref.shape[0]
    rows = lax.broadcasted_iota(jnp.int32, (size, size), 0)
    cols = lax.broadcasted_iota(jnp.int32, (size, size), 1)
    work = gram_ref[...]
    lower = jnp.zeros((size, size), jnp.float32)
    upper = jnp.zeros((size, size), jnp.float32)
    for j in range(size):
        pivot = jnp.sqrt(work[j : j + 1, j : j + 1])
        column = jnp.where(rows[:, j : j + 1] >= j, work[:, j : j + 1] / pivot, 0.0)
        row = jnp.where(cols[j : j + 1, :] >= j, work[j : j + 1, :] / pivot, 0.0)
        lower = jnp.where(cols == j, column, lower)
        upper = jnp.where(rows == j, row, upper)
        work = work - column * row
    pending = jnp.where(rows == cols, 1.0, 0.0).astype(jnp.float32)
    inverse = jnp.zeros((size, size), jnp.float32)
    for k in range(size):
        solved = pending[k : k + 1, :] / lower[k : k + 1, k : k + 1]
        inverse = jnp.where(rows == k, solved, inverse)
        below = jnp.where(rows[:, k : k + 1] > k, lower[:, k : k + 1], 0.0)
        pending = pending - below * solved
    upper_ref[...] = upper
    inverse_ref[...] = inverse


def cholesky_factors(gram, cells_total):
    size = gram.shape[0]
    square = jax.ShapeDtypeStruct((size, size), jnp.float32)
    scaled = gram / cells_total
    symmetric = (scaled + scaled.T) / 2
    return pl.pallas_call(factor_kernel, out_shape=[square, square])(symmetric)


def body(start_block, conductivity, reaction):
    cells_total = (
        start_block.shape[1]
        * start_block.shape[2]
        * start_block.shape[3]
        * lax.axis_size("gx")
        * lax.axis_size("gy")
    )
    rhs, depth, rows, cols = start_block.shape
    strips = halo_strips(start_block, conductivity, reaction)
    krylov = krylov_powers(start_block, conductivity, reaction, strips).reshape(COLS, -1)
    local_gram = jnp.dot(
        krylov, krylov.T, precision=lax.Precision.HIGHEST, preferred_element_type=jnp.float32
    )
    upper_first, inverse_first = cholesky_factors(tree_sum(local_gram, ("gx", "gy")), cells_total)
    first_q = jnp.dot(
        inverse_first, krylov, precision=lax.Precision.HIGHEST, preferred_element_type=jnp.float32
    )
    local_again = jnp.dot(
        first_q, first_q.T, precision=lax.Precision.HIGH, preferred_element_type=jnp.float32
    )
    upper_second, inverse_second = cholesky_factors(tree_sum(local_again, ("gx", "gy")), cells_total)
    basis = jnp.dot(
        inverse_second, first_q, precision=lax.Precision.HIGH, preferred_element_type=jnp.float32
    )
    r_factor = jnp.dot(
        upper_second,
        upper_first,
        precision=lax.Precision.HIGHEST,
        preferred_element_type=jnp.float32,
    )
    return (
        basis.reshape(COLS, start_block.shape[1], start_block.shape[2], start_block.shape[3]),
        r_factor,
        upper_first,
    )


def solution(mesh):
    return jax.shard_map(
        body,
        mesh=mesh,
        in_specs=(P(None, None, "gx", "gy"), P(None, "gx", "gy"), P(None, "gx", "gy")),
        out_specs=(P(None, None, "gx", "gy"), P(), P()),
        check_vma=False,
    )
```

```python
import jax
import jax.numpy as jnp
from jax import lax
from jax.sharding import PartitionSpec as P
from jax.experimental import pallas as pl
from jax.experimental.pallas import tpu as pltpu

STEPS = 4
COLS = 40


center_shift = 7.0
step_scale = 1.0 / 3.0


HALO = 4
LANES = 256


def edge_rows(start_block, conductivity, reaction, lo, hi):
    rhs, depth, rows, cols = start_block.shape
    return jnp.concatenate(
        [
            start_block[:, :, lo:hi].reshape(rhs * depth, hi - lo, cols),
            conductivity[:, lo:hi],
            reaction[:, lo:hi],
        ],
        axis=0,
    )


def shift_pairs(axis):
    count = lax.axis_size(axis)
    to_next = [(i, (i + 1) % count) for i in range(count)]
    return (to_next, [(j, i) for i, j in to_next])


def tall_plane(core, from_next, from_prev):
    return jnp.concatenate([core, from_next, from_prev], axis=0)


PACK = 32


def columns_kernel(block_ref, coef_ref, react_ref, xn_ref, xp_ref, first_ref, last_ref):
    rhs, depth, rows, cols = block_ref.shape
    width = xn_ref.shape[1]
    groups, tall_rows = first_ref.shape[:2]
    lane = lax.broadcasted_iota(jnp.int32, (tall_rows, cols), 1)
    cores = [block_ref[r, z] for r in range(rhs) for z in range(depth)]
    cores += [coef_ref[z] for z in range(depth)] + [react_ref[z] for z in range(depth)]
    for group in range(groups):
        first = jnp.zeros((tall_rows, cols), jnp.float32)
        last = jnp.zeros((tall_rows, cols), jnp.float32)
        for k in range(PACK):
            plane = group * PACK + k
            if plane >= len(cores):
                break
            tall = tall_plane(cores[plane], xn_ref[plane], xp_ref[plane])
            mine = (lane >= width * k) & (lane < width * (k + 1))
            first = jnp.where(mine, pltpu.roll(tall, width * k, 1), first)
            last = jnp.where(mine, pltpu.roll(tall, (width * (k + 1)) % cols, 1), last)
        first_ref[group] = first
        last_ref[group] = last


def edge_columns(start_block, conductivity, reaction, x_next, x_prev):
    planes, width, cols = x_next.shape
    rows = start_block.shape[2] + 2 * width
    whole = lambda shape: pl.BlockSpec(shape, lambda: (0,) * len(shape))
    strip = jax.ShapeDtypeStruct((-(-planes // PACK), rows, cols), jnp.float32)
    return pl.pallas_call(
        columns_kernel,
        in_specs=[
            whole(start_block.shape),
            whole(conductivity.shape),
            whole(reaction.shape),
            whole(x_next.shape),
            whole(x_prev.shape),
        ],
        out_specs=[whole(strip.shape), whole(strip.shape)],
        out_shape=[strip, strip],
    )(start_block, conductivity, reaction, x_next, x_prev)


def halo_strips(start_block, conductivity, reaction):
    rows = start_block.shape[2]
    x_next_pairs, x_prev_pairs = shift_pairs("gx")
    first = edge_rows(start_block, conductivity, reaction, 0, HALO)
    last = edge_rows(start_block, conductivity, reaction, rows - HALO, rows)
    x_next = lax.ppermute(first, "gx", x_prev_pairs)
    x_prev = lax.ppermute(last, "gx", x_next_pairs)
    first, last = edge_columns(start_block, conductivity, reaction, x_next, x_prev)
    y_next_pairs, y_prev_pairs = shift_pairs("gy")
    y_next = lax.ppermute(first, "gy", y_prev_pairs)
    y_prev = lax.ppermute(last, "gy", y_next_pairs)
    return (x_next, x_prev, y_next, y_prev)


def padded_plane(core, xn, xp, yn, yp, slot):
    tall = tall_plane(core, xn, xp)
    rows, cols = tall.shape
    width = xn.shape[0]
    lane = lax.broadcasted_iota(jnp.int32, (rows, cols), 1)
    from_next = pltpu.roll(yn, (cols - width * slot) % cols, 1)
    from_prev = pltpu.roll(yp, (cols - width - width * slot) % cols, 1)
    side = jnp.where(lane < width, from_next, jnp.where(lane >= cols - width, from_prev, 0.0))
    return jnp.concatenate([tall, side], axis=1)


def fold_pairs(count, stride, span, fold):
    pairs = []
    for i in range(count):
        place = (i // stride) % span
        other = (span - 1 - place) if fold else (place ^ 1)
        pairs.append((i, i + (other - place) * stride))
    return pairs


def ring_spans(axis):
    count = lax.axis_size(axis)
    rings = {("gx", 16): ((4, 4), (1, 4)), ("gy", 8): ((1, 2), (2, 4))}
    if (axis, count) in rings:
        return rings[(axis, count)]
    return tuple((1 << b, 2) for b in range(count.bit_length() - 1))


def tree_sum(value, axes):
    for axis in axes:
        count = lax.axis_size(axis)
        for stride, span in ring_spans(axis):
            folds = (False, True) if span == 4 else (False,)
            for fold in folds:
                value = value + lax.ppermute(value, axis, fold_pairs(count, stride, span, fold))
    return value


def neighbour(value, direction):
    axis, offset = direction
    if axis == 0:
        count = value.shape[0]
        cut = offset % count
        return jnp.concatenate([value[cut:], value[:cut]], axis=0)
    return pltpu.roll(value, (-offset) % value.shape[axis], axis)


DIRECTIONS = ((1, 1), (1, -1), (2, 1), (2, -1), (0, 1), (0, -1))


def powers_kernel(*refs):
    block_ref, coef_ref, react_ref = refs[:3]
    x_strips = refs[3:9]
    yn_ref, yp_ref = refs[9:11]
    out_ref, weight_ref, react_pad_ref = refs[11:14]
    buffers = refs[14:]
    depth, rows, cols = (out_ref.shape[2], out_ref.shape[3], out_ref.shape[4])
    r = pl.program_id(0)

    def planes(core_of, group, first_plane):
        xn, xp = (x_strips[2 * group], x_strips[2 * group + 1])
        stacked = []
        for z in range(depth):
            plane = first_plane + z
            tile = plane // PACK
            stacked.append(
                padded_plane(core_of(z), xn[z], xp[z], yn_ref[tile], yp_ref[tile], plane % PACK)
            )
        return jnp.stack(stacked, axis=0)

    rhs = pl.num_programs(0)

    @pl.when(r == 0)
    def _():
        coef = planes(lambda z: coef_ref[z], 1, rhs * depth)
        for d, direction in enumerate(DIRECTIONS):
            weight_ref[d] = 0.5 * (coef + neighbour(coef, direction))
        react_pad_ref[...] = planes(lambda z: react_ref[z], 2, rhs * depth + depth)

    out_ref[0, 0] = block_ref[0]
    buffers[0][...] = planes(lambda z: block_ref[0, z], 0, r * depth)
    for power in range(1, STEPS + 1):
        source, target = (buffers[(power - 1) % 2], buffers[power % 2])
        for z in range(depth):
            current = source[z]
            running = jnp.zeros_like(current)
            for d, (axis, offset) in enumerate(DIRECTIONS):
                if axis == 0:
                    beside = source[(z + offset) % depth]
                else:
                    beside = pltpu.roll(current, (-offset) % current.shape[axis - 1], axis - 1)
                running = running + weight_ref[d, z] * (current - beside)
            current = (react_pad_ref[z] * current + running - center_shift * current) * step_scale
            if power < STEPS:
                target[z] = current
            out_ref[power, 0, z] = current[:rows, :cols]


def krylov_powers(start_block, conductivity, reaction, strips):
    rhs, depth, rows, cols = start_block.shape
    x_next, x_prev, y_next, y_prev = strips
    width = x_next.shape[1]
    strip_specs = []
    for group in (lambda r: r, lambda r: rhs, lambda r: rhs + 1):
        for _ in range(2):
            strip_specs.append(pl.BlockSpec((depth, width, cols), lambda r, g=group: (g(r), 0, 0)))
    packed = pl.BlockSpec(y_next.shape, lambda r: (0, 0, 0))
    return pl.pallas_call(
        powers_kernel,
        grid=(rhs,),
        in_specs=[
            pl.BlockSpec((1, depth, rows, cols), lambda r: (r, 0, 0, 0)),
            pl.BlockSpec((depth, rows, cols), lambda r: (0, 0, 0)),
            pl.BlockSpec((depth, rows, cols), lambda r: (0, 0, 0)),
        ]
        + strip_specs
        + [packed, packed],
        out_specs=pl.BlockSpec((STEPS + 1, 1, depth, rows, cols), lambda r: (0, r, 0, 0, 0)),
        out_shape=jax.ShapeDtypeStruct((STEPS + 1, rhs, depth, rows, cols), jnp.float32),
        scratch_shapes=[
            pltpu.VMEM((len(DIRECTIONS), depth, rows + 2 * width, LANES), jnp.float32),
            pltpu.VMEM((depth, rows + 2 * width, LANES), jnp.float32),
            pltpu.VMEM((depth, rows + 2 * width, LANES), jnp.float32),
            pltpu.VMEM((depth, rows + 2 * width, LANES), jnp.float32),
        ],
        compiler_params=pltpu.CompilerParams(dimension_semantics=("arbitrary",)),
    )(start_block, conductivity, reaction, *([x_next, x_prev] * 3), y_next, y_prev)


def factor_kernel(gram_ref, upper_ref, inverse_ref):
    size = gram_ref.shape[0]
    rows = lax.broadcasted_iota(jnp.int32, (size, size), 0)
    cols = lax.broadcasted_iota(jnp.int32, (size, size), 1)
    work = gram_ref[...]
    lower = jnp.zeros((size, size), jnp.float32)
    upper = jnp.zeros((size, size), jnp.float32)
    for j in range(size):
        pivot = jnp.sqrt(work[j : j + 1, j : j + 1])
        column = jnp.where(rows[:, j : j + 1] >= j, work[:, j : j + 1] / pivot, 0.0)
        row = jnp.where(cols[j : j + 1, :] >= j, work[j : j + 1, :] / pivot, 0.0)
        lower = jnp.where(cols == j, column, lower)
        upper = jnp.where(rows == j, row, upper)
        work = work - column * row
    pending = jnp.where(rows == cols, 1.0, 0.0).astype(jnp.float32)
    inverse = jnp.zeros((size, size), jnp.float32)
    for k in range(size):
        solved = pending[k : k + 1, :] / lower[k : k + 1, k : k + 1]
        inverse = jnp.where(rows == k, solved, inverse)
        below = jnp.where(rows[:, k : k + 1] > k, lower[:, k : k + 1], 0.0)
        pending = pending - below * solved
    upper_ref[...] = upper
    inverse_ref[...] = inverse


def cholesky_factors(gram, cells_total):
    size = gram.shape[0]
    square = jax.ShapeDtypeStruct((size, size), jnp.float32)
    scaled = gram / cells_total
    symmetric = (scaled + scaled.T) / 2
    return pl.pallas_call(factor_kernel, out_shape=[square, square])(symmetric)


def body(start_block, conductivity, reaction):
    cells_total = (
        start_block.shape[1]
        * start_block.shape[2]
        * start_block.shape[3]
        * lax.axis_size("gx")
        * lax.axis_size("gy")
    )
    rhs, depth, rows, cols = start_block.shape
    strips = halo_strips(start_block, conductivity, reaction)
    krylov = krylov_powers(start_block, conductivity, reaction, strips).reshape(COLS, -1)
    local_gram = jnp.dot(
        krylov, krylov.T, precision=lax.Precision.HIGHEST, preferred_element_type=jnp.float32
    )
    upper_first, inverse_first = cholesky_factors(tree_sum(local_gram, ("gx", "gy")), cells_total)
    first_q = jnp.dot(
        inverse_first, krylov, precision=lax.Precision.HIGHEST, preferred_element_type=jnp.float32
    )
    local_again = jnp.dot(
        first_q, first_q.T, precision=lax.Precision.HIGH, preferred_element_type=jnp.float32
    )
    upper_second, inverse_second = cholesky_factors(tree_sum(local_again, ("gx", "gy")), cells_total)
    basis = jnp.dot(
        inverse_second, first_q, precision=lax.Precision.HIGH, preferred_element_type=jnp.float32
    )
    r_factor = jnp.dot(
        upper_second,
        upper_first,
        precision=lax.Precision.HIGHEST,
        preferred_element_type=jnp.float32,
    )
    return (
        basis.reshape(COLS, start_block.shape[1], start_block.shape[2], start_block.shape[3]),
        r_factor,
        upper_first,
    )


def solution(mesh):
    return jax.shard_map(
        body,
        mesh=mesh,
        in_specs=(P(None, None, "gx", "gy"), P(None, "gx", "gy"), P(None, "gx", "gy")),
        out_specs=(P(None, None, "gx", "gy"), P(), P()),
        check_vma=False,
    )
```

```python
import jax
import jax.numpy as jnp
from jax import lax
from jax.sharding import PartitionSpec as P
from jax.experimental import pallas as pl
from jax.experimental.pallas import tpu as pltpu

STEPS = 4
COLS = 40


center_shift = 7.0
step_scale = 1.0 / 3.0


HALO = 4
LANES = 256


def edge_rows(start_block, conductivity, reaction, lo, hi):
    rhs, depth, rows, cols = start_block.shape
    return jnp.concatenate(
        [
            start_block[:, :, lo:hi].reshape(rhs * depth, hi - lo, cols),
            conductivity[:, lo:hi],
            reaction[:, lo:hi],
        ],
        axis=0,
    )


def shift_pairs(axis):
    count = lax.axis_size(axis)
    to_next = [(i, (i + 1) % count) for i in range(count)]
    return (to_next, [(j, i) for i, j in to_next])


def tall_plane(core, from_next, from_prev):
    return jnp.concatenate([core, from_next, from_prev], axis=0)


PACK = 32


def columns_kernel(block_ref, coef_ref, react_ref, xn_ref, xp_ref, first_ref, last_ref):
    rhs, depth, rows, cols = block_ref.shape
    width = xn_ref.shape[1]
    groups, tall_rows = first_ref.shape[:2]
    lane = lax.broadcasted_iota(jnp.int32, (tall_rows, cols), 1)
    cores = [block_ref[r, z] for r in range(rhs) for z in range(depth)]
    cores += [coef_ref[z] for z in range(depth)] + [react_ref[z] for z in range(depth)]
    for group in range(groups):
        first = jnp.zeros((tall_rows, cols), jnp.float32)
        last = jnp.zeros((tall_rows, cols), jnp.float32)
        for k in range(PACK):
            plane = group * PACK + k
            if plane >= len(cores):
                break
            tall = tall_plane(cores[plane], xn_ref[plane], xp_ref[plane])
            mine = (lane >= width * k) & (lane < width * (k + 1))
            first = jnp.where(mine, pltpu.roll(tall, width * k, 1), first)
            last = jnp.where(mine, pltpu.roll(tall, (width * (k + 1)) % cols, 1), last)
        first_ref[group] = first
        last_ref[group] = last


def edge_columns(start_block, conductivity, reaction, x_next, x_prev):
    planes, width, cols = x_next.shape
    rows = start_block.shape[2] + 2 * width
    whole = lambda shape: pl.BlockSpec(shape, lambda: (0,) * len(shape))
    strip = jax.ShapeDtypeStruct((-(-planes // PACK), rows, cols), jnp.float32)
    return pl.pallas_call(
        columns_kernel,
        in_specs=[
            whole(start_block.shape),
            whole(conductivity.shape),
            whole(reaction.shape),
            whole(x_next.shape),
            whole(x_prev.shape),
        ],
        out_specs=[whole(strip.shape), whole(strip.shape)],
        out_shape=[strip, strip],
    )(start_block, conductivity, reaction, x_next, x_prev)


def halo_strips(start_block, conductivity, reaction):
    rows = start_block.shape[2]
    x_next_pairs, x_prev_pairs = shift_pairs("gx")
    first = edge_rows(start_block, conductivity, reaction, 0, HALO)
    last = edge_rows(start_block, conductivity, reaction, rows - HALO, rows)
    x_next = lax.ppermute(first, "gx", x_prev_pairs)
    x_prev = lax.ppermute(last, "gx", x_next_pairs)
    first, last = edge_columns(start_block, conductivity, reaction, x_next, x_prev)
    y_next_pairs, y_prev_pairs = shift_pairs("gy")
    y_next = lax.ppermute(first, "gy", y_prev_pairs)
    y_prev = lax.ppermute(last, "gy", y_next_pairs)
    return (x_next, x_prev, y_next, y_prev)


def padded_plane(core, xn, xp, yn, yp, slot):
    tall = tall_plane(core, xn, xp)
    rows, cols = tall.shape
    width = xn.shape[0]
    lane = lax.broadcasted_iota(jnp.int32, (rows, cols), 1)
    from_next = pltpu.roll(yn, (cols - width * slot) % cols, 1)
    from_prev = pltpu.roll(yp, (cols - width - width * slot) % cols, 1)
    side = jnp.where(lane < width, from_next, jnp.where(lane >= cols - width, from_prev, 0.0))
    return jnp.concatenate([tall, side], axis=1)


def fold_pairs(count, stride, span, fold):
    pairs = []
    for i in range(count):
        place = (i // stride) % span
        other = (span - 1 - place) if fold else (place ^ 1)
        pairs.append((i, i + (other - place) * stride))
    return pairs


def ring_spans(axis):
    count = lax.axis_size(axis)
    rings = {("gx", 16): ((4, 4), (1, 4)), ("gy", 8): ((1, 2), (2, 4))}
    if (axis, count) in rings:
        return rings[(axis, count)]
    return tuple((1 << b, 2) for b in range(count.bit_length() - 1))


def tree_sum(value, axes):
    for axis in axes:
        count = lax.axis_size(axis)
        for stride, span in ring_spans(axis):
            folds = (False, True) if span == 4 else (False,)
            for fold in folds:
                value = value + lax.ppermute(value, axis, fold_pairs(count, stride, span, fold))
    return value


def neighbour(value, direction):
    axis, offset = direction
    if axis == 0:
        count = value.shape[0]
        cut = offset % count
        return jnp.concatenate([value[cut:], value[:cut]], axis=0)
    return pltpu.roll(value, (-offset) % value.shape[axis], axis)


DIRECTIONS = ((1, 1), (1, -1), (2, 1), (2, -1), (0, 1), (0, -1))


def store_plane(out_ref, power, r, z, plane):
    rhs = pl.num_programs(0)
    rows = plane.shape[0]
    out_ref[power, pl.ds(z * rows * rhs + r, rows, stride=rhs), :] = plane


def powers_kernel(*refs):
    block_ref, coef_ref, react_ref = refs[:3]
    x_strips = refs[3:9]
    yn_ref, yp_ref = refs[9:11]
    out_ref, weight_ref, react_pad_ref = refs[11:14]
    buffers = refs[14:]
    depth, rows, cols = block_ref.shape[1:]
    r = pl.program_id(0)

    def planes(core_of, group, first_plane):
        xn, xp = (x_strips[2 * group], x_strips[2 * group + 1])
        stacked = []
        for z in range(depth):
            plane = first_plane + z
            tile = plane // PACK
            stacked.append(
                padded_plane(core_of(z), xn[z], xp[z], yn_ref[tile], yp_ref[tile], plane % PACK)
            )
        return jnp.stack(stacked, axis=0)

    rhs = pl.num_programs(0)

    @pl.when(r == 0)
    def _():
        coef = planes(lambda z: coef_ref[z], 1, rhs * depth)
        for d, direction in enumerate(DIRECTIONS):
            weight_ref[d] = 0.5 * (coef + neighbour(coef, direction))
        react_pad_ref[...] = planes(lambda z: react_ref[z], 2, rhs * depth + depth)

    for z in range(depth):
        store_plane(out_ref, 0, r, z, block_ref[0, z])
    buffers[0][...] = planes(lambda z: block_ref[0, z], 0, r * depth)
    for power in range(1, STEPS + 1):
        source, target = (buffers[(power - 1) % 2], buffers[power % 2])
        for z in range(depth):
            current = source[z]
            running = jnp.zeros_like(current)
            for d, (axis, offset) in enumerate(DIRECTIONS):
                if axis == 0:
                    beside = source[(z + offset) % depth]
                else:
                    beside = pltpu.roll(current, (-offset) % current.shape[axis - 1], axis - 1)
                running = running + weight_ref[d, z] * (current - beside)
            current = (react_pad_ref[z] * current + running - center_shift * current) * step_scale
            if power < STEPS:
                target[z] = current
            store_plane(out_ref, power, r, z, current[:rows, :cols])


def krylov_powers(start_block, conductivity, reaction, strips):
    rhs, depth, rows, cols = start_block.shape
    x_next, x_prev, y_next, y_prev = strips
    width = x_next.shape[1]
    strip_specs = []
    for group in (lambda r: r, lambda r: rhs, lambda r: rhs + 1):
        for _ in range(2):
            strip_specs.append(pl.BlockSpec((depth, width, cols), lambda r, g=group: (g(r), 0, 0)))
    packed = pl.BlockSpec(y_next.shape, lambda r: (0, 0, 0))
    return pl.pallas_call(
        powers_kernel,
        grid=(rhs,),
        in_specs=[
            pl.BlockSpec((1, depth, rows, cols), lambda r: (r, 0, 0, 0)),
            pl.BlockSpec((depth, rows, cols), lambda r: (0, 0, 0)),
            pl.BlockSpec((depth, rows, cols), lambda r: (0, 0, 0)),
        ]
        + strip_specs
        + [packed, packed],
        out_specs=pl.BlockSpec((STEPS + 1, depth * rows * rhs, cols), lambda r: (0, 0, 0)),
        out_shape=jax.ShapeDtypeStruct((STEPS + 1, depth * rows * rhs, cols), jnp.float32),
        scratch_shapes=[
            pltpu.VMEM((len(DIRECTIONS), depth, rows + 2 * width, LANES), jnp.float32),
            pltpu.VMEM((depth, rows + 2 * width, LANES), jnp.float32),
            pltpu.VMEM((depth, rows + 2 * width, LANES), jnp.float32),
            pltpu.VMEM((depth, rows + 2 * width, LANES), jnp.float32),
        ],
        compiler_params=pltpu.CompilerParams(dimension_semantics=("arbitrary",)),
    )(start_block, conductivity, reaction, *([x_next, x_prev] * 3), y_next, y_prev)


def factor_kernel(gram_ref, upper_ref, inverse_ref):
    size = gram_ref.shape[0]
    rows = lax.broadcasted_iota(jnp.int32, (size, size), 0)
    cols = lax.broadcasted_iota(jnp.int32, (size, size), 1)
    work = gram_ref[...]
    lower = jnp.zeros((size, size), jnp.float32)
    upper = jnp.zeros((size, size), jnp.float32)
    for j in range(size):
        pivot = jnp.sqrt(work[j : j + 1, j : j + 1])
        column = jnp.where(rows[:, j : j + 1] >= j, work[:, j : j + 1] / pivot, 0.0)
        row = jnp.where(cols[j : j + 1, :] >= j, work[j : j + 1, :] / pivot, 0.0)
        lower = jnp.where(cols == j, column, lower)
        upper = jnp.where(rows == j, row, upper)
        work = work - column * row
    pending = jnp.where(rows == cols, 1.0, 0.0).astype(jnp.float32)
    inverse = jnp.zeros((size, size), jnp.float32)
    for k in range(size):
        solved = pending[k : k + 1, :] / lower[k : k + 1, k : k + 1]
        inverse = jnp.where(rows == k, solved, inverse)
        below = jnp.where(rows[:, k : k + 1] > k, lower[:, k : k + 1], 0.0)
        pending = pending - below * solved
    upper_ref[...] = upper
    inverse_ref[...] = inverse


def cholesky_factors(gram, cells_total):
    size = gram.shape[0]
    square = jax.ShapeDtypeStruct((size, size), jnp.float32)
    scaled = gram / cells_total
    symmetric = (scaled + scaled.T) / 2
    return pl.pallas_call(factor_kernel, out_shape=[square, square])(symmetric)


def body(start_block, conductivity, reaction):
    cells_total = (
        start_block.shape[1]
        * start_block.shape[2]
        * start_block.shape[3]
        * lax.axis_size("gx")
        * lax.axis_size("gy")
    )
    rhs, depth, rows, cols = start_block.shape
    strips = halo_strips(start_block, conductivity, reaction)
    tiles = krylov_powers(start_block, conductivity, reaction, strips)
    krylov = (
        tiles.reshape(STEPS + 1, depth * rows, rhs, cols).transpose(0, 2, 1, 3).reshape(COLS, -1)
    )
    local_gram = jnp.dot(
        krylov, krylov.T, precision=lax.Precision.HIGHEST, preferred_element_type=jnp.float32
    )
    upper_first, inverse_first = cholesky_factors(tree_sum(local_gram, ("gx", "gy")), cells_total)
    first_q = jnp.dot(
        inverse_first, krylov, precision=lax.Precision.HIGHEST, preferred_element_type=jnp.float32
    )
    local_again = jnp.dot(
        first_q, first_q.T, precision=lax.Precision.HIGH, preferred_element_type=jnp.float32
    )
    upper_second, inverse_second = cholesky_factors(tree_sum(local_again, ("gx", "gy")), cells_total)
    basis = jnp.dot(
        inverse_second, first_q, precision=lax.Precision.HIGH, preferred_element_type=jnp.float32
    )
    r_factor = jnp.dot(
        upper_second,
        upper_first,
        precision=lax.Precision.HIGHEST,
        preferred_element_type=jnp.float32,
    )
    return (
        basis.reshape(COLS, start_block.shape[1], start_block.shape[2], start_block.shape[3]),
        r_factor,
        upper_first,
    )


def solution(mesh):
    return jax.shard_map(
        body,
        mesh=mesh,
        in_specs=(P(None, None, "gx", "gy"), P(None, "gx", "gy"), P(None, "gx", "gy")),
        out_specs=(P(None, None, "gx", "gy"), P(), P()),
        check_vma=False,
    )
```

```python
import jax
import jax.numpy as jnp
from jax import lax
from jax.sharding import PartitionSpec as P
from jax.experimental import pallas as pl
from jax.experimental.pallas import tpu as pltpu

STEPS = 4
COLS = 40


center_shift = 7.0
step_scale = 1.0 / 3.0


HALO = 4
LANES = 256


def edge_rows(start_block, conductivity, reaction, lo, hi):
    rhs, depth, rows, cols = start_block.shape
    return jnp.concatenate(
        [
            start_block[:, :, lo:hi].reshape(rhs * depth, hi - lo, cols),
            conductivity[:, lo:hi],
            reaction[:, lo:hi],
        ],
        axis=0,
    )


def shift_pairs(axis):
    count = lax.axis_size(axis)
    to_next = [(i, (i + 1) % count) for i in range(count)]
    return (to_next, [(j, i) for i, j in to_next])


def tall_plane(core, from_next, from_prev):
    return jnp.concatenate([core, from_next, from_prev], axis=0)


PACK = 32


def columns_kernel(block_ref, coef_ref, react_ref, xn_ref, xp_ref, first_ref, last_ref):
    rhs, depth, rows, cols = block_ref.shape
    width = xn_ref.shape[1]
    groups, tall_rows = first_ref.shape[:2]
    lane = lax.broadcasted_iota(jnp.int32, (tall_rows, cols), 1)
    cores = [block_ref[r, z] for r in range(rhs) for z in range(depth)]
    cores += [coef_ref[z] for z in range(depth)] + [react_ref[z] for z in range(depth)]
    for group in range(groups):
        first = jnp.zeros((tall_rows, cols), jnp.float32)
        last = jnp.zeros((tall_rows, cols), jnp.float32)
        for k in range(PACK):
            plane = group * PACK + k
            if plane >= len(cores):
                break
            tall = tall_plane(cores[plane], xn_ref[plane], xp_ref[plane])
            mine = (lane >= width * k) & (lane < width * (k + 1))
            first = jnp.where(mine, pltpu.roll(tall, width * k, 1), first)
            last = jnp.where(mine, pltpu.roll(tall, (width * (k + 1)) % cols, 1), last)
        first_ref[group] = first
        last_ref[group] = last


def edge_columns(start_block, conductivity, reaction, x_next, x_prev):
    planes, width, cols = x_next.shape
    rows = start_block.shape[2] + 2 * width
    whole = lambda shape: pl.BlockSpec(shape, lambda: (0,) * len(shape))
    strip = jax.ShapeDtypeStruct((-(-planes // PACK), rows, cols), jnp.float32)
    return pl.pallas_call(
        columns_kernel,
        in_specs=[
            whole(start_block.shape),
            whole(conductivity.shape),
            whole(reaction.shape),
            whole(x_next.shape),
            whole(x_prev.shape),
        ],
        out_specs=[whole(strip.shape), whole(strip.shape)],
        out_shape=[strip, strip],
    )(start_block, conductivity, reaction, x_next, x_prev)


def halo_strips(start_block, conductivity, reaction):
    rows = start_block.shape[2]
    x_next_pairs, x_prev_pairs = shift_pairs("gx")
    first = edge_rows(start_block, conductivity, reaction, 0, HALO)
    last = edge_rows(start_block, conductivity, reaction, rows - HALO, rows)
    x_next = lax.ppermute(first, "gx", x_prev_pairs)
    x_prev = lax.ppermute(last, "gx", x_next_pairs)
    first, last = edge_columns(start_block, conductivity, reaction, x_next, x_prev)
    y_next_pairs, y_prev_pairs = shift_pairs("gy")
    y_next = lax.ppermute(first, "gy", y_prev_pairs)
    y_prev = lax.ppermute(last, "gy", y_next_pairs)
    return (x_next, x_prev, y_next, y_prev)


def padded_plane(core, xn, xp, yn, yp, slot):
    tall = tall_plane(core, xn, xp)
    rows, cols = tall.shape
    width = xn.shape[0]
    lane = lax.broadcasted_iota(jnp.int32, (rows, cols), 1)
    from_next = pltpu.roll(yn, (cols - width * slot) % cols, 1)
    from_prev = pltpu.roll(yp, (cols - width - width * slot) % cols, 1)
    side = jnp.where(lane < width, from_next, jnp.where(lane >= cols - width, from_prev, 0.0))
    return jnp.concatenate([tall, side], axis=1)


def fold_pairs(count, stride, span, fold):
    pairs = []
    for i in range(count):
        place = (i // stride) % span
        other = (span - 1 - place) if fold else (place ^ 1)
        pairs.append((i, i + (other - place) * stride))
    return pairs


def ring_spans(axis):
    count = lax.axis_size(axis)
    rings = {("gx", 16): ((4, 4), (1, 4)), ("gy", 8): ((1, 2), (2, 4))}
    if (axis, count) in rings:
        return rings[(axis, count)]
    return tuple((1 << b, 2) for b in range(count.bit_length() - 1))


def tree_sum(value, axes):
    for axis in axes:
        count = lax.axis_size(axis)
        for stride, span in ring_spans(axis):
            folds = (False, True) if span == 4 else (False,)
            for fold in folds:
                value = value + lax.ppermute(value, axis, fold_pairs(count, stride, span, fold))
    return value


def neighbour(value, direction):
    axis, offset = direction
    if axis == 0:
        count = value.shape[0]
        cut = offset % count
        return jnp.concatenate([value[cut:], value[:cut]], axis=0)
    return pltpu.roll(value, (-offset) % value.shape[axis], axis)


DIRECTIONS = ((1, 1), (1, -1), (2, 1), (2, -1), (0, 1), (0, -1))


def store_plane(out_ref, power, r, z, plane):
    rhs = pl.num_programs(0)
    rows = plane.shape[0]
    out_ref[power, pl.ds(z * rows * rhs + r, rows, stride=rhs), :] = plane


def powers_kernel(*refs):
    block_ref, coef_ref, react_ref = refs[:3]
    x_strips = refs[3:9]
    yn_ref, yp_ref = refs[9:11]
    out_ref, weight_ref, react_pad_ref = refs[11:14]
    buffers = refs[14:]
    depth, rows, cols = block_ref.shape[1:]
    r = pl.program_id(0)

    def planes(core_of, group, first_plane):
        xn, xp = (x_strips[2 * group], x_strips[2 * group + 1])
        stacked = []
        for z in range(depth):
            plane = first_plane + z
            tile = plane // PACK
            stacked.append(
                padded_plane(core_of(z), xn[z], xp[z], yn_ref[tile], yp_ref[tile], plane % PACK)
            )
        return jnp.stack(stacked, axis=0)

    rhs = pl.num_programs(0)

    @pl.when(r == 0)
    def _():
        coef = planes(lambda z: coef_ref[z], 1, rhs * depth)
        for d, direction in enumerate(DIRECTIONS):
            weight_ref[d] = 0.5 * (coef + neighbour(coef, direction))
        react_pad_ref[...] = planes(lambda z: react_ref[z], 2, rhs * depth + depth)

    for z in range(depth):
        store_plane(out_ref, 0, r, z, block_ref[0, z])
    buffers[0][...] = planes(lambda z: block_ref[0, z], 0, r * depth)
    for power in range(1, STEPS + 1):
        source, target = (buffers[(power - 1) % 2], buffers[power % 2])
        keep = (slice(None), slice(None)) if power < STEPS else (slice(0, rows), slice(0, cols))
        for z in range(depth):
            whole = source[z]
            current = whole[keep]
            running = jnp.zeros_like(current)
            for d, (axis, offset) in enumerate(DIRECTIONS):
                if axis == 0:
                    beside = source[(z + offset) % depth][keep]
                else:
                    beside = pltpu.roll(whole, (-offset) % whole.shape[axis - 1], axis - 1)[keep]
                running = running + weight_ref[d, z][keep] * (current - beside)
            current = (react_pad_ref[z][keep] * current + running - center_shift * current) * step_scale
            if power < STEPS:
                target[z] = current
            store_plane(out_ref, power, r, z, current[:rows, :cols])


def krylov_powers(start_block, conductivity, reaction, strips):
    rhs, depth, rows, cols = start_block.shape
    x_next, x_prev, y_next, y_prev = strips
    width = x_next.shape[1]
    strip_specs = []
    for group in (lambda r: r, lambda r: rhs, lambda r: rhs + 1):
        for _ in range(2):
            strip_specs.append(pl.BlockSpec((depth, width, cols), lambda r, g=group: (g(r), 0, 0)))
    packed = pl.BlockSpec(y_next.shape, lambda r: (0, 0, 0))
    return pl.pallas_call(
        powers_kernel,
        grid=(rhs,),
        in_specs=[
            pl.BlockSpec((1, depth, rows, cols), lambda r: (r, 0, 0, 0)),
            pl.BlockSpec((depth, rows, cols), lambda r: (0, 0, 0)),
            pl.BlockSpec((depth, rows, cols), lambda r: (0, 0, 0)),
        ]
        + strip_specs
        + [packed, packed],
        out_specs=pl.BlockSpec((STEPS + 1, depth * rows * rhs, cols), lambda r: (0, 0, 0)),
        out_shape=jax.ShapeDtypeStruct((STEPS + 1, depth * rows * rhs, cols), jnp.float32),
        scratch_shapes=[
            pltpu.VMEM((len(DIRECTIONS), depth, rows + 2 * width, LANES), jnp.float32),
            pltpu.VMEM((depth, rows + 2 * width, LANES), jnp.float32),
            pltpu.VMEM((depth, rows + 2 * width, LANES), jnp.float32),
            pltpu.VMEM((depth, rows + 2 * width, LANES), jnp.float32),
        ],
        compiler_params=pltpu.CompilerParams(dimension_semantics=("arbitrary",)),
    )(start_block, conductivity, reaction, *([x_next, x_prev] * 3), y_next, y_prev)


def factor_kernel(gram_ref, upper_ref, inverse_ref):
    size = gram_ref.shape[0]
    rows = lax.broadcasted_iota(jnp.int32, (size, size), 0)
    cols = lax.broadcasted_iota(jnp.int32, (size, size), 1)
    work = gram_ref[...]
    lower = jnp.zeros((size, size), jnp.float32)
    upper = jnp.zeros((size, size), jnp.float32)
    for j in range(size):
        scale = 1.0 / jnp.sqrt(work[j : j + 1, j : j + 1])
        column = jnp.where(rows[:, j : j + 1] >= j, work[:, j : j + 1] * scale, 0.0)
        row = jnp.where(cols[j : j + 1, :] >= j, work[j : j + 1, :] * scale, 0.0)
        lower = jnp.where(cols == j, column, lower)
        upper = jnp.where(rows == j, row, upper)
        work = work - column * row
    pending = jnp.where(rows == cols, 1.0, 0.0).astype(jnp.float32)
    inverse = jnp.zeros((size, size), jnp.float32)
    for k in range(size):
        solved = pending[k : k + 1, :] * (1.0 / lower[k : k + 1, k : k + 1])
        inverse = jnp.where(rows == k, solved, inverse)
        below = jnp.where(rows[:, k : k + 1] > k, lower[:, k : k + 1], 0.0)
        pending = pending - below * solved
    upper_ref[...] = upper
    inverse_ref[...] = inverse


def cholesky_factors(gram, cells_total):
    size = gram.shape[0]
    square = jax.ShapeDtypeStruct((size, size), jnp.float32)
    scaled = gram / cells_total
    symmetric = (scaled + scaled.T) / 2
    return pl.pallas_call(factor_kernel, out_shape=[square, square])(symmetric)


def body(start_block, conductivity, reaction):
    cells_total = (
        start_block.shape[1]
        * start_block.shape[2]
        * start_block.shape[3]
        * lax.axis_size("gx")
        * lax.axis_size("gy")
    )
    rhs, depth, rows, cols = start_block.shape
    strips = halo_strips(start_block, conductivity, reaction)
    tiles = krylov_powers(start_block, conductivity, reaction, strips)
    krylov = (
        tiles.reshape(STEPS + 1, depth * rows, rhs, cols).transpose(0, 2, 1, 3).reshape(COLS, -1)
    )
    local_gram = jnp.dot(
        krylov, krylov.T, precision=lax.Precision.HIGHEST, preferred_element_type=jnp.float32
    )
    upper_first, inverse_first = cholesky_factors(tree_sum(local_gram, ("gx", "gy")), cells_total)
    first_q = jnp.dot(
        inverse_first, krylov, precision=lax.Precision.HIGHEST, preferred_element_type=jnp.float32
    )
    local_again = jnp.dot(
        first_q, first_q.T, precision=lax.Precision.HIGH, preferred_element_type=jnp.float32
    )
    upper_second, inverse_second = cholesky_factors(tree_sum(local_again, ("gx", "gy")), cells_total)
    basis = jnp.dot(
        inverse_second, first_q, precision=lax.Precision.HIGH, preferred_element_type=jnp.float32
    )
    r_factor = jnp.dot(
        upper_second,
        upper_first,
        precision=lax.Precision.HIGHEST,
        preferred_element_type=jnp.float32,
    )
    return (
        basis.reshape(COLS, start_block.shape[1], start_block.shape[2], start_block.shape[3]),
        r_factor,
        upper_first,
    )


def solution(mesh):
    return jax.shard_map(
        body,
        mesh=mesh,
        in_specs=(P(None, None, "gx", "gy"), P(None, "gx", "gy"), P(None, "gx", "gy")),
        out_specs=(P(None, None, "gx", "gy"), P(), P()),
        check_vma=False,
    )
```

```python
import jax
import jax.numpy as jnp
from jax import lax
from jax.sharding import PartitionSpec as P
from jax.experimental import pallas as pl
from jax.experimental.pallas import tpu as pltpu

STEPS = 4
COLS = 40


center_shift = 7.0
step_scale = 1.0 / 3.0


HALO = 4
LANES = 256


def edge_rows(start_block, conductivity, reaction, lo, hi):
    rhs, depth, rows, cols = start_block.shape
    return jnp.concatenate(
        [
            start_block[:, :, lo:hi].reshape(rhs * depth, hi - lo, cols),
            conductivity[:, lo:hi],
            reaction[:, lo:hi],
        ],
        axis=0,
    )


def shift_pairs(axis):
    count = lax.axis_size(axis)
    to_next = [(i, (i + 1) % count) for i in range(count)]
    return (to_next, [(j, i) for i, j in to_next])


def tall_plane(core, from_next, from_prev):
    spare = jnp.zeros_like(from_next)
    return jnp.concatenate([spare, from_prev, core, from_next, spare], axis=0)


PACK = 32
SKIRT = 8


def columns_kernel(block_ref, coef_ref, react_ref, xn_ref, xp_ref, first_ref, last_ref):
    rhs, depth, rows, cols = block_ref.shape
    width = xn_ref.shape[1]
    groups, tall_rows = first_ref.shape[:2]
    lane = lax.broadcasted_iota(jnp.int32, (tall_rows, cols), 1)
    cores = [block_ref[r, z] for r in range(rhs) for z in range(depth)]
    cores += [coef_ref[z] for z in range(depth)] + [react_ref[z] for z in range(depth)]
    for group in range(groups):
        first = jnp.zeros((tall_rows, cols), jnp.float32)
        last = jnp.zeros((tall_rows, cols), jnp.float32)
        for k in range(PACK):
            plane = group * PACK + k
            if plane >= len(cores):
                break
            tall = tall_plane(cores[plane], xn_ref[plane], xp_ref[plane])
            mine = (lane >= width * k) & (lane < width * (k + 1))
            first = jnp.where(mine, pltpu.roll(tall, width * k, 1), first)
            last = jnp.where(mine, pltpu.roll(tall, (width * (k + 1)) % cols, 1), last)
        first_ref[group] = first
        last_ref[group] = last


def edge_columns(start_block, conductivity, reaction, x_next, x_prev):
    planes, width, cols = x_next.shape
    rows = start_block.shape[2] + 4 * width
    whole = lambda shape: pl.BlockSpec(shape, lambda: (0,) * len(shape))
    strip = jax.ShapeDtypeStruct((-(-planes // PACK), rows, cols), jnp.float32)
    return pl.pallas_call(
        columns_kernel,
        in_specs=[
            whole(start_block.shape),
            whole(conductivity.shape),
            whole(reaction.shape),
            whole(x_next.shape),
            whole(x_prev.shape),
        ],
        out_specs=[whole(strip.shape), whole(strip.shape)],
        out_shape=[strip, strip],
    )(start_block, conductivity, reaction, x_next, x_prev)


def halo_strips(start_block, conductivity, reaction):
    rows = start_block.shape[2]
    x_next_pairs, x_prev_pairs = shift_pairs("gx")
    first = edge_rows(start_block, conductivity, reaction, 0, HALO)
    last = edge_rows(start_block, conductivity, reaction, rows - HALO, rows)
    x_next = lax.ppermute(first, "gx", x_prev_pairs)
    x_prev = lax.ppermute(last, "gx", x_next_pairs)
    first, last = edge_columns(start_block, conductivity, reaction, x_next, x_prev)
    y_next_pairs, y_prev_pairs = shift_pairs("gy")
    y_next = lax.ppermute(first, "gy", y_prev_pairs)
    y_prev = lax.ppermute(last, "gy", y_next_pairs)
    return (x_next, x_prev, y_next, y_prev)


def padded_plane(core, xn, xp, yn, yp, slot):
    tall = tall_plane(core, xn, xp)
    rows, cols = tall.shape
    width = xn.shape[0]
    lane = lax.broadcasted_iota(jnp.int32, (rows, cols), 1)
    from_next = pltpu.roll(yn, (cols - width * slot) % cols, 1)
    from_prev = pltpu.roll(yp, (cols - width - width * slot) % cols, 1)
    side = jnp.where(lane < width, from_next, jnp.where(lane >= cols - width, from_prev, 0.0))
    return jnp.concatenate([tall, side], axis=1)


def fold_pairs(count, stride, span, fold):
    pairs = []
    for i in range(count):
        place = (i // stride) % span
        other = (span - 1 - place) if fold else (place ^ 1)
        pairs.append((i, i + (other - place) * stride))
    return pairs


def ring_spans(axis):
    count = lax.axis_size(axis)
    rings = {("gx", 16): ((4, 4), (1, 4)), ("gy", 8): ((1, 2), (2, 4))}
    if (axis, count) in rings:
        return rings[(axis, count)]
    return tuple((1 << b, 2) for b in range(count.bit_length() - 1))


def tree_sum(value, axes):
    for axis in axes:
        count = lax.axis_size(axis)
        for stride, span in ring_spans(axis):
            folds = (False, True) if span == 4 else (False,)
            for fold in folds:
                value = value + lax.ppermute(value, axis, fold_pairs(count, stride, span, fold))
    return value


def neighbour(value, direction):
    axis, offset = direction
    if axis == 0:
        count = value.shape[0]
        cut = offset % count
        return jnp.concatenate([value[cut:], value[:cut]], axis=0)
    return pltpu.roll(value, (-offset) % value.shape[axis], axis)


DIRECTIONS = ((1, 1), (1, -1), (2, 1), (2, -1), (0, 1), (0, -1))


def store_plane(out_ref, power, r, z, plane):
    rhs = pl.num_programs(0)
    rows = plane.shape[0]
    out_ref[power, pl.ds(z * rows * rhs + r, rows, stride=rhs), :] = plane


def powers_kernel(*refs):
    block_ref, coef_ref, react_ref = refs[:3]
    x_strips = refs[3:9]
    yn_ref, yp_ref = refs[9:11]
    out_ref, weight_ref, react_pad_ref = refs[11:14]
    buffers = refs[14:]
    depth, rows, cols = block_ref.shape[1:]
    r = pl.program_id(0)
    tall = weight_ref.shape[2]
    lead = (tall - rows) // 2

    def planes(core_of, group, first_plane):
        xn, xp = (x_strips[2 * group], x_strips[2 * group + 1])
        stacked = []
        for z in range(depth):
            plane = first_plane + z
            tile = plane // PACK
            stacked.append(
                padded_plane(core_of(z), xn[z], xp[z], yn_ref[tile], yp_ref[tile], plane % PACK)
            )
        return jnp.stack(stacked, axis=0)

    rhs = pl.num_programs(0)

    @pl.when(r == 0)
    def _():
        coef = planes(lambda z: coef_ref[z], 1, rhs * depth)
        for d, direction in enumerate(DIRECTIONS):
            weight_ref[d] = 0.5 * (coef + neighbour(coef, direction))
        react_pad_ref[...] = planes(lambda z: react_ref[z], 2, rhs * depth + depth)
        for buffer in buffers:
            buffer[:, :SKIRT] = jnp.zeros((depth, SKIRT, LANES), jnp.float32)
            buffer[:, SKIRT + tall :] = jnp.zeros((depth, SKIRT, LANES), jnp.float32)

    for z in range(depth):
        store_plane(out_ref, 0, r, z, block_ref[0, z])
    buffers[0][:, SKIRT : SKIRT + tall] = planes(lambda z: block_ref[0, z], 0, r * depth)
    for power in range(1, STEPS + 1):
        source, target = (buffers[(power - 1) % 2], buffers[power % 2])
        first, count = (0, tall) if power < STEPS else (lead, rows)
        top = SKIRT + first
        for z in range(depth):
            current = source[z, top : top + count]
            sides = {
                (1, 1): source[z, top + 1 : top + 1 + count],
                (1, -1): source[z, top - 1 : top - 1 + count],
                (0, 1): source[(z + 1) % depth, top : top + count],
                (0, -1): source[(z - 1) % depth, top : top + count],
            }
            running = jnp.zeros_like(current)
            for d, (axis, offset) in enumerate(DIRECTIONS):
                if axis == 2:
                    beside = pltpu.roll(current, (-offset) % LANES, 1)
                else:
                    beside = sides[(axis, offset)]
                running = running + weight_ref[d, z, first : first + count] * (current - beside)
            current = (
                react_pad_ref[z, first : first + count] * current + running - center_shift * current
            ) * step_scale
            if power < STEPS:
                target[z, SKIRT : SKIRT + tall] = current
                store_plane(out_ref, power, r, z, current[lead : lead + rows, :cols])
            else:
                store_plane(out_ref, power, r, z, current[:, :cols])


def krylov_powers(start_block, conductivity, reaction, strips):
    rhs, depth, rows, cols = start_block.shape
    x_next, x_prev, y_next, y_prev = strips
    width = x_next.shape[1]
    strip_specs = []
    for group in (lambda r: r, lambda r: rhs, lambda r: rhs + 1):
        for _ in range(2):
            strip_specs.append(pl.BlockSpec((depth, width, cols), lambda r, g=group: (g(r), 0, 0)))
    packed = pl.BlockSpec(y_next.shape, lambda r: (0, 0, 0))
    return pl.pallas_call(
        powers_kernel,
        grid=(rhs,),
        in_specs=[
            pl.BlockSpec((1, depth, rows, cols), lambda r: (r, 0, 0, 0)),
            pl.BlockSpec((depth, rows, cols), lambda r: (0, 0, 0)),
            pl.BlockSpec((depth, rows, cols), lambda r: (0, 0, 0)),
        ]
        + strip_specs
        + [packed, packed],
        out_specs=pl.BlockSpec((STEPS + 1, depth * rows * rhs, cols), lambda r: (0, 0, 0)),
        out_shape=jax.ShapeDtypeStruct((STEPS + 1, depth * rows * rhs, cols), jnp.float32),
        scratch_shapes=[
            pltpu.VMEM((len(DIRECTIONS), depth, rows + 4 * width, LANES), jnp.float32),
            pltpu.VMEM((depth, rows + 4 * width, LANES), jnp.float32),
            pltpu.VMEM((depth, rows + 4 * width + 2 * SKIRT, LANES), jnp.float32),
            pltpu.VMEM((depth, rows + 4 * width + 2 * SKIRT, LANES), jnp.float32),
        ],
        compiler_params=pltpu.CompilerParams(dimension_semantics=("arbitrary",)),
    )(start_block, conductivity, reaction, *([x_next, x_prev] * 3), y_next, y_prev)


def factor_kernel(gram_ref, upper_ref, inverse_ref):
    size = gram_ref.shape[0]
    rows = lax.broadcasted_iota(jnp.int32, (size, size), 0)
    cols = lax.broadcasted_iota(jnp.int32, (size, size), 1)
    work = gram_ref[...]
    lower = jnp.zeros((size, size), jnp.float32)
    upper = jnp.zeros((size, size), jnp.float32)
    for j in range(size):
        scale = 1.0 / jnp.sqrt(work[j : j + 1, j : j + 1])
        column = jnp.where(rows[:, j : j + 1] >= j, work[:, j : j + 1] * scale, 0.0)
        row = jnp.where(cols[j : j + 1, :] >= j, work[j : j + 1, :] * scale, 0.0)
        lower = jnp.where(cols == j, column, lower)
        upper = jnp.where(rows == j, row, upper)
        work = work - column * row
    pending = jnp.where(rows == cols, 1.0, 0.0).astype(jnp.float32)
    inverse = jnp.zeros((size, size), jnp.float32)
    for k in range(size):
        solved = pending[k : k + 1, :] * (1.0 / lower[k : k + 1, k : k + 1])
        inverse = jnp.where(rows == k, solved, inverse)
        below = jnp.where(rows[:, k : k + 1] > k, lower[:, k : k + 1], 0.0)
        pending = pending - below * solved
    upper_ref[...] = upper
    inverse_ref[...] = inverse


def cholesky_factors(gram, cells_total):
    size = gram.shape[0]
    square = jax.ShapeDtypeStruct((size, size), jnp.float32)
    scaled = gram / cells_total
    symmetric = (scaled + scaled.T) / 2
    return pl.pallas_call(factor_kernel, out_shape=[square, square])(symmetric)


def body(start_block, conductivity, reaction):
    cells_total = (
        start_block.shape[1]
        * start_block.shape[2]
        * start_block.shape[3]
        * lax.axis_size("gx")
        * lax.axis_size("gy")
    )
    rhs, depth, rows, cols = start_block.shape
    strips = halo_strips(start_block, conductivity, reaction)
    tiles = krylov_powers(start_block, conductivity, reaction, strips)
    krylov = (
        tiles.reshape(STEPS + 1, depth * rows, rhs, cols).transpose(0, 2, 1, 3).reshape(COLS, -1)
    )
    local_gram = jnp.dot(
        krylov, krylov.T, precision=lax.Precision.HIGHEST, preferred_element_type=jnp.float32
    )
    upper_first, inverse_first = cholesky_factors(tree_sum(local_gram, ("gx", "gy")), cells_total)
    first_q = jnp.dot(
        inverse_first, krylov, precision=lax.Precision.HIGHEST, preferred_element_type=jnp.float32
    )
    local_again = jnp.dot(
        first_q, first_q.T, precision=lax.Precision.HIGH, preferred_element_type=jnp.float32
    )
    upper_second, inverse_second = cholesky_factors(tree_sum(local_again, ("gx", "gy")), cells_total)
    basis = jnp.dot(
        inverse_second, first_q, precision=lax.Precision.HIGH, preferred_element_type=jnp.float32
    )
    r_factor = jnp.dot(
        upper_second,
        upper_first,
        precision=lax.Precision.HIGHEST,
        preferred_element_type=jnp.float32,
    )
    return (
        basis.reshape(COLS, start_block.shape[1], start_block.shape[2], start_block.shape[3]),
        r_factor,
        upper_first,
    )


def solution(mesh):
    return jax.shard_map(
        body,
        mesh=mesh,
        in_specs=(P(None, None, "gx", "gy"), P(None, "gx", "gy"), P(None, "gx", "gy")),
        out_specs=(P(None, None, "gx", "gy"), P(), P()),
        check_vma=False,
    )
```

```python
import jax
import jax.numpy as jnp
from jax import lax
from jax.sharding import PartitionSpec as P
from jax.experimental import pallas as pl
from jax.experimental.pallas import tpu as pltpu

STEPS = 4
COLS = 40


center_shift = 7.0
step_scale = 1.0 / 3.0


HALO = 4
LANES = 256


def edge_rows(start_block, conductivity, reaction, lo, hi):
    rhs, depth, rows, cols = start_block.shape
    return jnp.concatenate(
        [
            start_block[:, :, lo:hi].reshape(rhs * depth, hi - lo, cols),
            conductivity[:, lo:hi],
            reaction[:, lo:hi],
        ],
        axis=0,
    )


def shift_pairs(axis):
    count = lax.axis_size(axis)
    to_next = [(i, (i + 1) % count) for i in range(count)]
    return (to_next, [(j, i) for i, j in to_next])


def tall_plane(core, from_next, from_prev):
    return jnp.concatenate([core, from_next, from_prev], axis=0)


PACK = 32


def columns_kernel(block_ref, coef_ref, react_ref, xn_ref, xp_ref, first_ref, last_ref):
    rhs, depth, rows, cols = block_ref.shape
    width = xn_ref.shape[1]
    groups, tall_rows = first_ref.shape[:2]
    lane = lax.broadcasted_iota(jnp.int32, (tall_rows, cols), 1)
    cores = [block_ref[r, z] for r in range(rhs) for z in range(depth)]
    cores += [coef_ref[z] for z in range(depth)] + [react_ref[z] for z in range(depth)]
    for group in range(groups):
        first = jnp.zeros((tall_rows, cols), jnp.float32)
        last = jnp.zeros((tall_rows, cols), jnp.float32)
        for k in range(PACK):
            plane = group * PACK + k
            if plane >= len(cores):
                break
            tall = tall_plane(cores[plane], xn_ref[plane], xp_ref[plane])
            mine = (lane >= width * k) & (lane < width * (k + 1))
            first = jnp.where(mine, pltpu.roll(tall, width * k, 1), first)
            last = jnp.where(mine, pltpu.roll(tall, (width * (k + 1)) % cols, 1), last)
        first_ref[group] = first
        last_ref[group] = last


def edge_columns(start_block, conductivity, reaction, x_next, x_prev):
    planes, width, cols = x_next.shape
    rows = start_block.shape[2] + 2 * width
    whole = lambda shape: pl.BlockSpec(shape, lambda: (0,) * len(shape))
    strip = jax.ShapeDtypeStruct((-(-planes // PACK), rows, cols), jnp.float32)
    return pl.pallas_call(
        columns_kernel,
        in_specs=[
            whole(start_block.shape),
            whole(conductivity.shape),
            whole(reaction.shape),
            whole(x_next.shape),
            whole(x_prev.shape),
        ],
        out_specs=[whole(strip.shape), whole(strip.shape)],
        out_shape=[strip, strip],
    )(start_block, conductivity, reaction, x_next, x_prev)


def halo_strips(start_block, conductivity, reaction):
    rows = start_block.shape[2]
    x_next_pairs, x_prev_pairs = shift_pairs("gx")
    first = edge_rows(start_block, conductivity, reaction, 0, HALO)
    last = edge_rows(start_block, conductivity, reaction, rows - HALO, rows)
    x_next = lax.ppermute(first, "gx", x_prev_pairs)
    x_prev = lax.ppermute(last, "gx", x_next_pairs)
    first, last = edge_columns(start_block, conductivity, reaction, x_next, x_prev)
    y_next_pairs, y_prev_pairs = shift_pairs("gy")
    y_next = lax.ppermute(first, "gy", y_prev_pairs)
    y_prev = lax.ppermute(last, "gy", y_next_pairs)
    return (x_next, x_prev, y_next, y_prev)


def padded_plane(core, xn, xp, yn, yp, slot):
    tall = tall_plane(core, xn, xp)
    rows, cols = tall.shape
    width = xn.shape[0]
    lane = lax.broadcasted_iota(jnp.int32, (rows, cols), 1)
    from_next = pltpu.roll(yn, (cols - width * slot) % cols, 1)
    from_prev = pltpu.roll(yp, (cols - width - width * slot) % cols, 1)
    side = jnp.where(lane < width, from_next, jnp.where(lane >= cols - width, from_prev, 0.0))
    return jnp.concatenate([tall, side], axis=1)


def fold_pairs(count, stride, span, fold):
    pairs = []
    for i in range(count):
        place = (i // stride) % span
        other = (span - 1 - place) if fold else (place ^ 1)
        pairs.append((i, i + (other - place) * stride))
    return pairs


def ring_spans(axis):
    count = lax.axis_size(axis)
    rings = {("gx", 16): ((4, 4), (1, 4)), ("gy", 8): ((1, 2), (2, 4))}
    if (axis, count) in rings:
        return rings[(axis, count)]
    return tuple((1 << b, 2) for b in range(count.bit_length() - 1))


def tree_sum(value, axes):
    for axis in axes:
        count = lax.axis_size(axis)
        for stride, span in ring_spans(axis):
            folds = (False, True) if span == 4 else (False,)
            for fold in folds:
                value = value + lax.ppermute(value, axis, fold_pairs(count, stride, span, fold))
    return value


def neighbour(value, direction):
    axis, offset = direction
    if axis == 0:
        count = value.shape[0]
        cut = offset % count
        return jnp.concatenate([value[cut:], value[:cut]], axis=0)
    return pltpu.roll(value, (-offset) % value.shape[axis], axis)


DIRECTIONS = ((1, 1), (1, -1), (2, 1), (2, -1), (0, 1), (0, -1))


def store_plane(out_ref, power, r, z, plane):
    rhs = pl.num_programs(0)
    rows = plane.shape[0]
    out_ref[power, pl.ds(z * rows * rhs + r, rows, stride=rhs), :] = plane


def powers_kernel(*refs):
    block_ref, coef_ref, react_ref = refs[:3]
    x_strips = refs[3:9]
    yn_ref, yp_ref = refs[9:11]
    out_ref, weight_ref, react_pad_ref = refs[11:14]
    buffers = refs[14:]
    depth, rows, cols = block_ref.shape[1:]
    r = pl.program_id(0)

    def planes(core_of, group, first_plane):
        xn, xp = (x_strips[2 * group], x_strips[2 * group + 1])
        stacked = []
        for z in range(depth):
            plane = first_plane + z
            tile = plane // PACK
            stacked.append(
                padded_plane(core_of(z), xn[z], xp[z], yn_ref[tile], yp_ref[tile], plane % PACK)
            )
        return jnp.stack(stacked, axis=0)

    rhs = pl.num_programs(0)

    @pl.when(r == 0)
    def _():
        coef = planes(lambda z: coef_ref[z], 1, rhs * depth)
        for d, direction in enumerate(DIRECTIONS):
            weight_ref[d] = 0.5 * (coef + neighbour(coef, direction))
        react_pad_ref[...] = planes(lambda z: react_ref[z], 2, rhs * depth + depth)

    for z in range(depth):
        store_plane(out_ref, 0, r, z, block_ref[0, z])
    buffers[0][...] = planes(lambda z: block_ref[0, z], 0, r * depth)
    for power in range(1, STEPS + 1):
        source, target = (buffers[(power - 1) % 2], buffers[power % 2])
        keep = (slice(None), slice(None)) if power < STEPS else (slice(0, rows), slice(0, cols))
        for z in range(depth):
            whole = source[z]
            current = whole[keep]
            running = jnp.zeros_like(current)
            for d, (axis, offset) in enumerate(DIRECTIONS):
                if axis == 0:
                    beside = source[(z + offset) % depth][keep]
                else:
                    beside = pltpu.roll(whole, (-offset) % whole.shape[axis - 1], axis - 1)[keep]
                running = running + weight_ref[d, z][keep] * (current - beside)
            current = (react_pad_ref[z][keep] * current + running - center_shift * current) * step_scale
            if power < STEPS:
                target[z] = current
            store_plane(out_ref, power, r, z, current[:rows, :cols])


def krylov_powers(start_block, conductivity, reaction, strips):
    rhs, depth, rows, cols = start_block.shape
    x_next, x_prev, y_next, y_prev = strips
    width = x_next.shape[1]
    strip_specs = []
    for group in (lambda r: r, lambda r: rhs, lambda r: rhs + 1):
        for _ in range(2):
            strip_specs.append(pl.BlockSpec((depth, width, cols), lambda r, g=group: (g(r), 0, 0)))
    packed = pl.BlockSpec(y_next.shape, lambda r: (0, 0, 0))
    return pl.pallas_call(
        powers_kernel,
        grid=(rhs,),
        in_specs=[
            pl.BlockSpec((1, depth, rows, cols), lambda r: (r, 0, 0, 0)),
            pl.BlockSpec((depth, rows, cols), lambda r: (0, 0, 0)),
            pl.BlockSpec((depth, rows, cols), lambda r: (0, 0, 0)),
        ]
        + strip_specs
        + [packed, packed],
        out_specs=pl.BlockSpec((STEPS + 1, depth * rows * rhs, cols), lambda r: (0, 0, 0)),
        out_shape=jax.ShapeDtypeStruct((STEPS + 1, depth * rows * rhs, cols), jnp.float32),
        scratch_shapes=[
            pltpu.VMEM((len(DIRECTIONS), depth, rows + 2 * width, LANES), jnp.float32),
            pltpu.VMEM((depth, rows + 2 * width, LANES), jnp.float32),
            pltpu.VMEM((depth, rows + 2 * width, LANES), jnp.float32),
            pltpu.VMEM((depth, rows + 2 * width, LANES), jnp.float32),
        ],
        compiler_params=pltpu.CompilerParams(dimension_semantics=("arbitrary",)),
    )(start_block, conductivity, reaction, *([x_next, x_prev] * 3), y_next, y_prev)


def factor_kernel(gram_ref, upper_ref, inverse_ref):
    size = gram_ref.shape[0]
    rows = lax.broadcasted_iota(jnp.int32, (size, size), 0)
    cols = lax.broadcasted_iota(jnp.int32, (size, size), 1)
    work = gram_ref[...]
    lower = jnp.zeros((size, size), jnp.float32)
    upper = jnp.zeros((size, size), jnp.float32)
    pending = jnp.where(rows == cols, 1.0, 0.0).astype(jnp.float32)
    inverse = jnp.zeros((size, size), jnp.float32)
    for j in range(size):
        scale = 1.0 / jnp.sqrt(work[j : j + 1, j : j + 1])
        column = jnp.where(rows[:, j : j + 1] >= j, work[:, j : j + 1] * scale, 0.0)
        row = jnp.where(cols[j : j + 1, :] >= j, work[j : j + 1, :] * scale, 0.0)
        lower = jnp.where(cols == j, column, lower)
        upper = jnp.where(rows == j, row, upper)
        work = work - column * row
        solved = pending[j : j + 1, :] * (1.0 / column[j : j + 1, :])
        inverse = jnp.where(rows == j, solved, inverse)
        below = jnp.where(rows[:, j : j + 1] > j, column, 0.0)
        pending = pending - below * solved
    upper_ref[...] = upper
    inverse_ref[...] = inverse


def cholesky_factors(gram, cells_total):
    size = gram.shape[0]
    square = jax.ShapeDtypeStruct((size, size), jnp.float32)
    scaled = gram / cells_total
    symmetric = (scaled + scaled.T) / 2
    return pl.pallas_call(factor_kernel, out_shape=[square, square])(symmetric)


def body(start_block, conductivity, reaction):
    cells_total = (
        start_block.shape[1]
        * start_block.shape[2]
        * start_block.shape[3]
        * lax.axis_size("gx")
        * lax.axis_size("gy")
    )
    rhs, depth, rows, cols = start_block.shape
    strips = halo_strips(start_block, conductivity, reaction)
    tiles = krylov_powers(start_block, conductivity, reaction, strips)
    krylov = (
        tiles.reshape(STEPS + 1, depth * rows, rhs, cols).transpose(0, 2, 1, 3).reshape(COLS, -1)
    )
    local_gram = jnp.dot(
        krylov, krylov.T, precision=lax.Precision.HIGHEST, preferred_element_type=jnp.float32
    )
    upper_first, inverse_first = cholesky_factors(tree_sum(local_gram, ("gx", "gy")), cells_total)
    first_q = jnp.dot(
        inverse_first, krylov, precision=lax.Precision.HIGHEST, preferred_element_type=jnp.float32
    )
    local_again = jnp.dot(
        first_q, first_q.T, precision=lax.Precision.HIGH, preferred_element_type=jnp.float32
    )
    upper_second, inverse_second = cholesky_factors(tree_sum(local_again, ("gx", "gy")), cells_total)
    basis = jnp.dot(
        inverse_second, first_q, precision=lax.Precision.HIGH, preferred_element_type=jnp.float32
    )
    r_factor = jnp.dot(
        upper_second,
        upper_first,
        precision=lax.Precision.HIGHEST,
        preferred_element_type=jnp.float32,
    )
    return (
        basis.reshape(COLS, start_block.shape[1], start_block.shape[2], start_block.shape[3]),
        r_factor,
        upper_first,
    )


def solution(mesh):
    return jax.shard_map(
        body,
        mesh=mesh,
        in_specs=(P(None, None, "gx", "gy"), P(None, "gx", "gy"), P(None, "gx", "gy")),
        out_specs=(P(None, None, "gx", "gy"), P(), P()),
        check_vma=False,
    )
```

```python
import functools

import jax
import jax.numpy as jnp
from jax import lax
from jax.sharding import PartitionSpec as P
from jax.experimental import pallas as pl
from jax.experimental.pallas import tpu as pltpu

STEPS = 4
COLS = 40


center_shift = 7.0
step_scale = 1.0 / 3.0


HALO = 4
LANES = 256


def edge_rows(start_block, conductivity, reaction, lo, hi):
    rhs, depth, rows, cols = start_block.shape
    return jnp.concatenate(
        [
            start_block[:, :, lo:hi].reshape(rhs * depth, hi - lo, cols),
            conductivity[:, lo:hi],
            reaction[:, lo:hi],
        ],
        axis=0,
    )


def shift_pairs(axis):
    count = lax.axis_size(axis)
    to_next = [(i, (i + 1) % count) for i in range(count)]
    return (to_next, [(j, i) for i, j in to_next])


def tall_plane(core, from_next, from_prev):
    return jnp.concatenate([core, from_next, from_prev], axis=0)


PACK = 32


def columns_kernel(block_ref, coef_ref, react_ref, xn_ref, xp_ref, first_ref, last_ref):
    rhs, depth, rows, cols = block_ref.shape
    width = xn_ref.shape[1]
    groups, tall_rows = first_ref.shape[:2]
    lane = lax.broadcasted_iota(jnp.int32, (tall_rows, cols), 1)
    cores = [block_ref[r, z] for r in range(rhs) for z in range(depth)]
    cores += [coef_ref[z] for z in range(depth)] + [react_ref[z] for z in range(depth)]
    for group in range(groups):
        first = jnp.zeros((tall_rows, cols), jnp.float32)
        last = jnp.zeros((tall_rows, cols), jnp.float32)
        for k in range(PACK):
            plane = group * PACK + k
            if plane >= len(cores):
                break
            tall = tall_plane(cores[plane], xn_ref[plane], xp_ref[plane])
            mine = (lane >= width * k) & (lane < width * (k + 1))
            first = jnp.where(mine, pltpu.roll(tall, width * k, 1), first)
            last = jnp.where(mine, pltpu.roll(tall, (width * (k + 1)) % cols, 1), last)
        first_ref[group] = first
        last_ref[group] = last


def edge_columns(start_block, conductivity, reaction, x_next, x_prev):
    planes, width, cols = x_next.shape
    rows = start_block.shape[2] + 2 * width
    whole = lambda shape: pl.BlockSpec(shape, lambda: (0,) * len(shape))
    strip = jax.ShapeDtypeStruct((-(-planes // PACK), rows, cols), jnp.float32)
    return pl.pallas_call(
        columns_kernel,
        in_specs=[
            whole(start_block.shape),
            whole(conductivity.shape),
            whole(reaction.shape),
            whole(x_next.shape),
            whole(x_prev.shape),
        ],
        out_specs=[whole(strip.shape), whole(strip.shape)],
        out_shape=[strip, strip],
    )(start_block, conductivity, reaction, x_next, x_prev)


def halo_strips(start_block, conductivity, reaction):
    rows = start_block.shape[2]
    x_next_pairs, x_prev_pairs = shift_pairs("gx")
    first = edge_rows(start_block, conductivity, reaction, 0, HALO)
    last = edge_rows(start_block, conductivity, reaction, rows - HALO, rows)
    x_next = lax.ppermute(first, "gx", x_prev_pairs)
    x_prev = lax.ppermute(last, "gx", x_next_pairs)
    first, last = edge_columns(start_block, conductivity, reaction, x_next, x_prev)
    y_next_pairs, y_prev_pairs = shift_pairs("gy")
    y_next = lax.ppermute(first, "gy", y_prev_pairs)
    y_prev = lax.ppermute(last, "gy", y_next_pairs)
    return (x_next, x_prev, y_next, y_prev)


def padded_plane(core, xn, xp, yn, yp, slot):
    tall = tall_plane(core, xn, xp)
    rows, cols = tall.shape
    width = xn.shape[0]
    lane = lax.broadcasted_iota(jnp.int32, (rows, cols), 1)
    from_next = pltpu.roll(yn, (cols - width * slot) % cols, 1)
    from_prev = pltpu.roll(yp, (cols - width - width * slot) % cols, 1)
    side = jnp.where(lane < width, from_next, jnp.where(lane >= cols - width, from_prev, 0.0))
    return jnp.concatenate([tall, side], axis=1)


def fold_pairs(count, stride, span, fold):
    pairs = []
    for i in range(count):
        place = (i // stride) % span
        other = (span - 1 - place) if fold else (place ^ 1)
        pairs.append((i, i + (other - place) * stride))
    return pairs


def ring_spans(axis):
    count = lax.axis_size(axis)
    rings = {("gx", 16): ((4, 4), (1, 4)), ("gy", 8): ((1, 2), (2, 4))}
    if (axis, count) in rings:
        return rings[(axis, count)]
    return tuple((1 << b, 2) for b in range(count.bit_length() - 1))


def tree_sum(value, axes):
    for axis in axes:
        count = lax.axis_size(axis)
        for stride, span in ring_spans(axis):
            folds = (False, True) if span == 4 else (False,)
            for fold in folds:
                value = value + lax.ppermute(value, axis, fold_pairs(count, stride, span, fold))
    return value


def neighbour(value, direction):
    axis, offset = direction
    if axis == 0:
        count = value.shape[0]
        cut = offset % count
        return jnp.concatenate([value[cut:], value[:cut]], axis=0)
    return pltpu.roll(value, (-offset) % value.shape[axis], axis)


DIRECTIONS = ((1, 1), (1, -1), (2, 1), (2, -1), (0, 1), (0, -1))


def store_plane(out_ref, power, r, z, plane):
    rhs = pl.num_programs(0)
    rows = plane.shape[0]
    out_ref[power, pl.ds(z * rows * rhs + r, rows, stride=rhs), :] = plane


def powers_kernel(*refs):
    block_ref, coef_ref, react_ref = refs[:3]
    x_strips = refs[3:9]
    yn_ref, yp_ref = refs[9:11]
    out_ref, weight_ref, react_pad_ref = refs[11:14]
    buffers = refs[14:]
    depth, rows, cols = block_ref.shape[1:]
    r = pl.program_id(0)

    def planes(core_of, group, first_plane):
        xn, xp = (x_strips[2 * group], x_strips[2 * group + 1])
        stacked = []
        for z in range(depth):
            plane = first_plane + z
            tile = plane // PACK
            stacked.append(
                padded_plane(core_of(z), xn[z], xp[z], yn_ref[tile], yp_ref[tile], plane % PACK)
            )
        return jnp.stack(stacked, axis=0)

    rhs = pl.num_programs(0)

    @pl.when(r == 0)
    def _():
        coef = planes(lambda z: coef_ref[z], 1, rhs * depth)
        for d, direction in enumerate(DIRECTIONS):
            weight_ref[d] = 0.5 * (coef + neighbour(coef, direction))
        react_pad_ref[...] = planes(lambda z: react_ref[z], 2, rhs * depth + depth)

    for z in range(depth):
        store_plane(out_ref, 0, r, z, block_ref[0, z])
    buffers[0][...] = planes(lambda z: block_ref[0, z], 0, r * depth)
    for power in range(1, STEPS + 1):
        source, target = (buffers[(power - 1) % 2], buffers[power % 2])
        keep = (slice(None), slice(None)) if power < STEPS else (slice(0, rows), slice(0, cols))
        for z in range(depth):
            whole = source[z]
            current = whole[keep]
            running = jnp.zeros_like(current)
            for d, (axis, offset) in enumerate(DIRECTIONS):
                if axis == 0:
                    beside = source[(z + offset) % depth][keep]
                else:
                    beside = pltpu.roll(whole, (-offset) % whole.shape[axis - 1], axis - 1)[keep]
                running = running + weight_ref[d, z][keep] * (current - beside)
            current = (react_pad_ref[z][keep] * current + running - center_shift * current) * step_scale
            if power < STEPS:
                target[z] = current
            store_plane(out_ref, power, r, z, current[:rows, :cols])


def krylov_powers(start_block, conductivity, reaction, strips):
    rhs, depth, rows, cols = start_block.shape
    x_next, x_prev, y_next, y_prev = strips
    width = x_next.shape[1]
    strip_specs = []
    for group in (lambda r: r, lambda r: rhs, lambda r: rhs + 1):
        for _ in range(2):
            strip_specs.append(pl.BlockSpec((depth, width, cols), lambda r, g=group: (g(r), 0, 0)))
    packed = pl.BlockSpec(y_next.shape, lambda r: (0, 0, 0))
    return pl.pallas_call(
        powers_kernel,
        grid=(rhs,),
        in_specs=[
            pl.BlockSpec((1, depth, rows, cols), lambda r: (r, 0, 0, 0)),
            pl.BlockSpec((depth, rows, cols), lambda r: (0, 0, 0)),
            pl.BlockSpec((depth, rows, cols), lambda r: (0, 0, 0)),
        ]
        + strip_specs
        + [packed, packed],
        out_specs=pl.BlockSpec((STEPS + 1, depth * rows * rhs, cols), lambda r: (0, 0, 0)),
        out_shape=jax.ShapeDtypeStruct((STEPS + 1, depth * rows * rhs, cols), jnp.float32),
        scratch_shapes=[
            pltpu.VMEM((len(DIRECTIONS), depth, rows + 2 * width, LANES), jnp.float32),
            pltpu.VMEM((depth, rows + 2 * width, LANES), jnp.float32),
            pltpu.VMEM((depth, rows + 2 * width, LANES), jnp.float32),
            pltpu.VMEM((depth, rows + 2 * width, LANES), jnp.float32),
        ],
        compiler_params=pltpu.CompilerParams(dimension_semantics=("arbitrary",)),
    )(start_block, conductivity, reaction, *([x_next, x_prev] * 3), y_next, y_prev)


def factor_kernel(gram_ref, upper_ref, inverse_ref, *, cells_total):
    size = gram_ref.shape[0]
    rows = lax.broadcasted_iota(jnp.int32, (size, size), 0)
    cols = lax.broadcasted_iota(jnp.int32, (size, size), 1)
    scaled = gram_ref[...] / cells_total
    wide = LANES // 2
    tile = jnp.zeros((wide, wide), jnp.float32)
    tile = jnp.concatenate(
        [jnp.concatenate([scaled, jnp.zeros((size, wide - size), jnp.float32)], axis=1), tile[size:]], axis=0
    )
    work = (scaled + tile.T[:size, :size]) / 2
    lower = jnp.zeros((size, size), jnp.float32)
    upper = jnp.zeros((size, size), jnp.float32)
    for j in range(size):
        scale = 1.0 / jnp.sqrt(work[j : j + 1, j : j + 1])
        column = jnp.where(rows[:, j : j + 1] >= j, work[:, j : j + 1] * scale, 0.0)
        row = jnp.where(cols[j : j + 1, :] >= j, work[j : j + 1, :] * scale, 0.0)
        lower = jnp.where(cols == j, column, lower)
        upper = jnp.where(rows == j, row, upper)
        work = work - column * row
    pending = jnp.where(rows == cols, 1.0, 0.0).astype(jnp.float32)
    inverse = jnp.zeros((size, size), jnp.float32)
    for k in range(size):
        solved = pending[k : k + 1, :] * (1.0 / lower[k : k + 1, k : k + 1])
        inverse = jnp.where(rows == k, solved, inverse)
        below = jnp.where(rows[:, k : k + 1] > k, lower[:, k : k + 1], 0.0)
        pending = pending - below * solved
    upper_ref[...] = upper
    inverse_ref[...] = inverse


def cholesky_factors(gram, cells_total):
    size = gram.shape[0]
    square = jax.ShapeDtypeStruct((size, size), jnp.float32)
    kernel = functools.partial(factor_kernel, cells_total=float(cells_total))
    return pl.pallas_call(kernel, out_shape=[square, square])(gram)


def body(start_block, conductivity, reaction):
    cells_total = (
        start_block.shape[1]
        * start_block.shape[2]
        * start_block.shape[3]
        * lax.axis_size("gx")
        * lax.axis_size("gy")
    )
    rhs, depth, rows, cols = start_block.shape
    strips = halo_strips(start_block, conductivity, reaction)
    tiles = krylov_powers(start_block, conductivity, reaction, strips)
    krylov = (
        tiles.reshape(STEPS + 1, depth * rows, rhs, cols).transpose(0, 2, 1, 3).reshape(COLS, -1)
    )
    local_gram = jnp.dot(
        krylov, krylov.T, precision=lax.Precision.HIGHEST, preferred_element_type=jnp.float32
    )
    upper_first, inverse_first = cholesky_factors(tree_sum(local_gram, ("gx", "gy")), cells_total)
    first_q = jnp.dot(
        inverse_first, krylov, precision=lax.Precision.HIGHEST, preferred_element_type=jnp.float32
    )
    local_again = jnp.dot(
        first_q, first_q.T, precision=lax.Precision.HIGH, preferred_element_type=jnp.float32
    )
    upper_second, inverse_second = cholesky_factors(tree_sum(local_again, ("gx", "gy")), cells_total)
    basis = jnp.dot(
        inverse_second, first_q, precision=lax.Precision.HIGH, preferred_element_type=jnp.float32
    )
    r_factor = jnp.dot(
        upper_second,
        upper_first,
        precision=lax.Precision.HIGHEST,
        preferred_element_type=jnp.float32,
    )
    return (
        basis.reshape(COLS, start_block.shape[1], start_block.shape[2], start_block.shape[3]),
        r_factor,
        upper_first,
    )


def solution(mesh):
    return jax.shard_map(
        body,
        mesh=mesh,
        in_specs=(P(None, None, "gx", "gy"), P(None, "gx", "gy"), P(None, "gx", "gy")),
        out_specs=(P(None, None, "gx", "gy"), P(), P()),
        check_vma=False,
    )
```
